32 devices in a mesh: wide: 8 (over z, y), narrow: 4 (over x, core).
Axes of the slice: x: 2, y: 2, z: 4, core: 2. Of those that a mesh axis runs over, the one named last changes fastest.
Arguments:
- spectra: bfloat16 [512, 2, 8192], P('wide'), may hold values from -6 to 6
- band_gain: float32 [8192], replicated, may hold values from 0.1 to 1.9
- owners: int32 [2], replicated, may hold values from 0 to 7
- pair_near: int32 [8, 2, 512], P('wide', None, 'narrow'), may hold values from 0 to 63
- pair_far: int32 [8, 2, 512], P('wide', None, 'narrow'), may hold values from 0 to 63
- stack_bins: int32 [8, 2, 512], P('wide', None, 'narrow'), may hold values from 0 to 255, as said below
Outputs:
- stacked: float32 [4, 64, 1024], P('narrow', 'wide')
The draws below stay inside these ranges and needn't reach their ends.
Inputs may be any that keep to these rules, and one draw needn't show every extreme that they name: `stack_bins`: bins n * 64 to (n + 1) * 64 - 1 belong to narrow index n. Of the 256 rows of one device (steps together), at most 128 have bins of one narrow index; in every draw some narrow index gets exactly 128 rows from each device of its group.
All inputs are finite; a program needn't handle non-finite values.
Results may differ from the reference program's by a relative error of at most 0.0036.
Values may be sent and summed in bfloat16 or wider, within the bound.
No kernel may reach another device: no remote copies, remote signals or barrier semaphores. Data moves between devices by JAX's collectives and lax.ppermute only.
A program may use at most 128 MiB of HBM per device.

```python
import jax
import jax.numpy as jnp
from jax import lax

F = 8192
LAGS = 1024
BLK = 64
STEPS = 2
PAIRS = 128
GW = 8
CHAN = 512
N_WIDE = 8
N_NARROW = 4


def draw_stack_bins(key, part):
    rows_each = STEPS * PAIRS
    capacity = STEPS * PAIRS // 2
    bins_each = GW * N_WIDE
    device_count = N_WIDE * N_NARROW
    hot_key, order_key, other_key, within_key = jax.random.split(key, 4)
    hot_owner = jax.random.randint(hot_key, (N_WIDE, 1), 0, N_NARROW)
    hot_each = jnp.repeat(hot_owner, N_NARROW, axis=0)
    order_keys = jax.random.split(order_key, device_count)
    ranks = jax.vmap(lambda single: jax.random.permutation(single, rows_each))(order_keys)
    others = jax.random.randint(other_key, (device_count, rows_each), 0, N_NARROW - 1)
    owner_ids = jnp.where(ranks < capacity, hot_each, (hot_each + 1 + others) % N_NARROW)
    within = jax.random.randint(within_key, (device_count, rows_each), 0, bins_each)
    bin_ids = owner_ids * bins_each + within
    bin_ids = bin_ids.reshape(N_WIDE, N_NARROW, STEPS, PAIRS).transpose(0, 2, 1, 3)
    return bin_ids.reshape(N_WIDE, STEPS, N_NARROW * PAIRS).astype(jnp.int32)


def plant(values, key, least, top_value):
    index_at = [jax.random.randint(jax.random.fold_in(key, axis), (), 0, length) for axis, length in enumerate(values.shape)]
    widest = values.shape.index(max(values.shape))
    next_to = index_at[:widest] + [(index_at[widest] + 1) % values.shape[widest]] + index_at[widest + 1:]
    return values.at[tuple(index_at)].set(least).at[tuple(next_to)].set(top_value)


def block_levels(stream_key, extent, pieces, least, high):
    def one(position, parts):
        draws = jax.random.uniform(jax.random.fold_in(jax.random.fold_in(stream_key, 6), position), (parts,), jnp.float32, least / len(pieces), high / len(pieces))
        return jnp.repeat(jnp.exp(draws), extent[position] // parts).reshape((-1,) + (1,) * (len(extent) - position - 1))

    gain = one(*pieces[0])
    for cut in pieces[1:]:
        gain = gain * one(*cut)
    return gain


def gaussian(key, shape, width, reach, cuts=(), kind=jnp.bfloat16):
    loudness = block_levels(key, shape, cuts, -0.22, 0.18) if cuts else 1.0
    drawn = jax.random.normal(key, shape, jnp.float32) * width * loudness
    return jnp.minimum(jnp.maximum(drawn, -reach), reach).astype(kind)


def setup_inputs(seed: int = 0) -> dict:
    key_of = jax.random.split(jax.random.key(seed), 7)
    spectra = gaussian(key_of[0], (CHAN, 2, F), 1.0, 6.0, ((0, 8),))
    band_gain = jnp.clip(1.0 + 0.18 * jax.random.normal(key_of[1], (F,), jnp.float32), 0.1, 1.9)
    owners = jax.random.randint(key_of[2], (STEPS,), 0, N_WIDE).astype(jnp.int32)
    pair_near = plant(jax.random.randint(key_of[3], (N_WIDE, STEPS, N_NARROW * PAIRS), 0, BLK), jax.random.fold_in(key_of[3], 1), 0, BLK - 1).astype(jnp.int32)
    pair_far = plant(jax.random.randint(key_of[4], (N_WIDE, STEPS, N_NARROW * PAIRS), 0, BLK), jax.random.fold_in(key_of[4], 1), 0, BLK - 1).astype(jnp.int32)
    stack_bins = draw_stack_bins(jax.random.fold_in(key_of[6], 71), 0)
    return dict(spectra=spectra, band_gain=band_gain, owners=owners, pair_near=pair_near, pair_far=pair_far, stack_bins=stack_bins)


def lag_table(freqs, lag_count):
    freq_index = jnp.arange(freqs, dtype=jnp.int32)[:, None]
    lag_index = jnp.arange(lag_count, dtype=jnp.int32)[None, :] - lag_count // 2
    turns = (freq_index * lag_index) % (2 * freqs)
    phase = turns.astype(jnp.float32) * (jnp.pi / freqs)
    cosine = jnp.cos(phase).astype(jnp.bfloat16)
    minus_sine = (-jnp.sin(phase)).astype(jnp.bfloat16)
    return jnp.concatenate([cosine, minus_sine], axis=0)


def cross_rows(near_rows, far_rows, band_gain):
    near_real = near_rows[:, 0].astype(jnp.float32)
    near_imag = near_rows[:, 1].astype(jnp.float32)
    far_real = far_rows[:, 0].astype(jnp.float32)
    far_imag = far_rows[:, 1].astype(jnp.float32)
    real_part = (near_real * far_real + near_imag * far_imag) * band_gain
    imag_part = (near_imag * far_real - near_real * far_imag) * band_gain
    return jnp.concatenate([real_part, imag_part], axis=1).astype(jnp.bfloat16)


def reference(spectra, band_gain, owners, pair_near, pair_far, stack_bins):
    lag_matrix = lag_table(F, LAGS)
    blocks = spectra.reshape(N_WIDE, BLK, 2, F)
    total_bins = N_NARROW * GW * N_WIDE
    inv_root = 1.0 / (F ** 0.5)
    stacked = jnp.zeros((total_bins, LAGS), jnp.float32)
    for step_index in range(STEPS):
        far_block = blocks[owners[step_index]]

        def per_wide(running, wide_index, step_index=step_index, far_block=far_block):
            near_block = blocks[wide_index]
            near_rows = near_block[pair_near[wide_index, step_index]]
            far_rows = far_block[pair_far[wide_index, step_index]]
            cross_part = cross_rows(near_rows, far_rows, band_gain)
            lagged = jnp.dot(cross_part, lag_matrix, preferred_element_type=jnp.float32) * inv_root
            added = jax.ops.segment_sum(lagged, stack_bins[wide_index, step_index], num_segments=total_bins)
            return running + added, None

        stacked, _ = lax.scan(per_wide, stacked, jnp.arange(N_WIDE, dtype=jnp.int32))
    stack_scale = (GW / (STEPS * PAIRS)) ** 0.5
    return (stacked * stack_scale).reshape(N_NARROW, GW * N_WIDE, LAGS)
```

```python
import jax
import jax.numpy as jnp
from jax import lax
from jax.sharding import PartitionSpec as P

LAGS = 1024
GW = 8


def trig_pair(freq_values, lag_values, freqs):
    turns = freq_values[:, None] * lag_values[None, :] % (2 * freqs)
    phase = turns.astype(jnp.float32) * (jnp.pi / freqs)
    return (jnp.cos(phase), jnp.sin(phase))


def lag_rows(first_freq, row_count, freqs, lag_count):
    unit_size = 64
    lag_values = jnp.arange(lag_count, dtype=jnp.int32) - lag_count // 2
    coarse_freq = first_freq + jnp.arange(row_count // unit_size, dtype=jnp.int32) * unit_size
    fine_freq = jnp.arange(unit_size, dtype=jnp.int32)
    coarse_cos, coarse_sin = trig_pair(coarse_freq, lag_values, freqs)
    fine_cos, fine_sin = trig_pair(fine_freq, lag_values, freqs)
    cosine = (
        coarse_cos[:, None, :] * fine_cos[None, :, :]
        - coarse_sin[:, None, :] * fine_sin[None, :, :]
    )
    sine = (
        coarse_sin[:, None, :] * fine_cos[None, :, :]
        + coarse_cos[:, None, :] * fine_sin[None, :, :]
    )
    cosine = cosine.reshape(row_count, lag_count).astype(jnp.bfloat16)
    minus_sine = (-sine).reshape(row_count, lag_count).astype(jnp.bfloat16)
    return jnp.concatenate([cosine, minus_sine], axis=0)


def select_rows(block, indices):
    block_rows = block.shape[0]
    flat_block = block.reshape(block_rows, -1)
    picker = (indices[:, None] == jnp.arange(block_rows, dtype=jnp.int32)[None, :]).astype(
        jnp.bfloat16
    )
    chosen = jnp.dot(picker, flat_block, preferred_element_type=jnp.bfloat16)
    return chosen.reshape(indices.shape[0], 2, -1)


def cross_rows(near_rows, far_rows, band_gain):
    near_real = near_rows[:, 0].astype(jnp.float32)
    near_imag = near_rows[:, 1].astype(jnp.float32)
    far_real = far_rows[:, 0].astype(jnp.float32)
    far_imag = far_rows[:, 1].astype(jnp.float32)
    real_part = (near_real * far_real + near_imag * far_imag) * band_gain
    imag_part = (near_imag * far_real - near_real * far_imag) * band_gain
    return jnp.concatenate([real_part, imag_part], axis=1).astype(jnp.bfloat16)


def local(spectra, band_gain, owners, pair_near, pair_far, stack_bins):
    narrow_count = lax.axis_size("narrow")
    wide_count = lax.axis_size("wide")
    narrow_index = lax.axis_index("narrow")
    block_rows, _, freqs = spectra.shape
    steps = owners.shape[0]
    share = freqs // narrow_count
    piece = share // wide_count
    total_bins = narrow_count * wide_count * GW
    first_freq = narrow_index * share

    near = lax.dynamic_slice_in_dim(spectra, first_freq, share, axis=2)
    gain = lax.dynamic_slice_in_dim(band_gain, first_freq, share, axis=0)

    with jax.named_scope("owner_share_exchange"):
        outgoing = near.reshape(block_rows, 2, wide_count, piece).transpose(2, 0, 1, 3)
        arrived = lax.all_to_all(outgoing, "wide", split_axis=0, concat_axis=0, tiled=True)
        chosen = jnp.stack(
            [lax.dynamic_index_in_dim(arrived, owners[s], 0, keepdims=False) for s in range(steps)]
        )
        gathered = lax.all_gather(chosen, "wide", axis=0, tiled=False)

    near_ids = lax.all_gather(pair_near[0], "narrow", axis=1, tiled=True)
    far_ids = lax.all_gather(pair_far[0], "narrow", axis=1, tiled=True)
    bin_ids = lax.all_gather(stack_bins[0], "narrow", axis=1, tiled=True).reshape(-1)

    with jax.named_scope("cross_spectra"):
        pieces = []
        for s in range(steps):
            far = gathered[:, s].transpose(1, 2, 0, 3).reshape(block_rows, 2, share)
            near_rows = select_rows(near, near_ids[s])
            far_rows = select_rows(far, far_ids[s])
            pieces.append(cross_rows(near_rows, far_rows, gain))
        cross_part = jnp.concatenate(pieces, axis=0)

    with jax.named_scope("lag_product"):
        lag_matrix = lag_rows(first_freq, share, freqs, LAGS)
        lagged = jnp.dot(cross_part, lag_matrix, preferred_element_type=jnp.float32)

    with jax.named_scope("bin_sums"):
        bin_hits = (
            jnp.arange(total_bins, dtype=jnp.int32)[:, None] == bin_ids[None, :]
        ).astype(jnp.float32)
        binned = jnp.dot(bin_hits, lagged, precision=lax.Precision.HIGHEST)
        binned = binned.reshape(narrow_count * wide_count, GW, LAGS)
        owned = lax.all_to_all(
            binned, ("narrow", "wide"), split_axis=0, concat_axis=0, tiled=True
        )
        stacked = jnp.sum(owned, axis=0)

    inv_root = 1.0 / freqs**0.5
    stack_scale = (GW / (steps * pair_near.shape[2])) ** 0.5
    return (stacked * (inv_root * stack_scale))[None]


def solution(mesh):
    in_specs = (
        P("wide", None, None),
        P(),
        P(),
        P("wide", None, "narrow"),
        P("wide", None, "narrow"),
        P("wide", None, "narrow"),
    )
    out_specs = P("narrow", "wide", None)
    return jax.shard_map(local, mesh=mesh, in_specs=in_specs, out_specs=out_specs, check_vma=False)
```

```python
import jax
import jax.numpy as jnp
from jax import lax
from jax.sharding import PartitionSpec as P

LAGS = 1024
GW = 8


def trig_pair(freq_values, lag_values, freqs):
    turns = freq_values[:, None] * lag_values[None, :] % (2 * freqs)
    phase = turns.astype(jnp.float32) * (jnp.pi / freqs)
    return (jnp.cos(phase), jnp.sin(phase))


def lag_rows(first_freq, row_count, freqs, lag_count):
    unit_size = 64
    lag_values = jnp.arange(lag_count, dtype=jnp.int32) - lag_count // 2
    coarse_freq = first_freq + jnp.arange(row_count // unit_size, dtype=jnp.int32) * unit_size
    fine_freq = jnp.arange(unit_size, dtype=jnp.int32)
    coarse_cos, coarse_sin = trig_pair(coarse_freq, lag_values, freqs)
    fine_cos, fine_sin = trig_pair(fine_freq, lag_values, freqs)
    cosine = (
        coarse_cos[:, None, :] * fine_cos[None, :, :]
        - coarse_sin[:, None, :] * fine_sin[None, :, :]
    )
    sine = (
        coarse_sin[:, None, :] * fine_cos[None, :, :]
        + coarse_cos[:, None, :] * fine_sin[None, :, :]
    )
    cosine = cosine.reshape(row_count, lag_count).astype(jnp.bfloat16)
    minus_sine = (-sine).reshape(row_count, lag_count).astype(jnp.bfloat16)
    return jnp.concatenate([cosine, minus_sine], axis=0)


def select_rows(block, indices):
    block_rows = block.shape[0]
    flat_block = block.reshape(block_rows, -1)
    picker = (indices[:, None] == jnp.arange(block_rows, dtype=jnp.int32)[None, :]).astype(
        jnp.bfloat16
    )
    chosen = jnp.dot(picker, flat_block, preferred_element_type=jnp.bfloat16)
    return chosen.reshape(indices.shape[0], 2, -1)


def cross_rows(near_rows, far_rows, band_gain):
    near_real = near_rows[:, 0].astype(jnp.float32)
    near_imag = near_rows[:, 1].astype(jnp.float32)
    far_real = far_rows[:, 0].astype(jnp.float32)
    far_imag = far_rows[:, 1].astype(jnp.float32)
    real_part = (near_real * far_real + near_imag * far_imag) * band_gain
    imag_part = (near_imag * far_real - near_real * far_imag) * band_gain
    return jnp.concatenate([real_part, imag_part], axis=1).astype(jnp.bfloat16)


def local(spectra, band_gain, owners, pair_near, pair_far, stack_bins):
    narrow_count = lax.axis_size("narrow")
    wide_count = lax.axis_size("wide")
    narrow_index = lax.axis_index("narrow")
    block_rows, _, freqs = spectra.shape
    steps = owners.shape[0]
    share = freqs // narrow_count
    piece = share // wide_count
    total_bins = narrow_count * wide_count * GW
    first_freq = narrow_index * share

    near = lax.dynamic_slice_in_dim(spectra, first_freq, share, axis=2)
    gain = lax.dynamic_slice_in_dim(band_gain, first_freq, share, axis=0)

    with jax.named_scope("owner_share_exchange"):
        outgoing = near.reshape(block_rows, 2, wide_count, piece).transpose(2, 0, 1, 3)
        arrived = lax.all_to_all(outgoing, "wide", split_axis=0, concat_axis=0, tiled=True)
        chosen = jnp.stack(
            [lax.dynamic_index_in_dim(arrived, owners[s], 0, keepdims=False) for s in range(steps)]
        )
        copies = jnp.broadcast_to(chosen[None], (wide_count,) + chosen.shape)
        gathered = lax.all_to_all(copies, "wide", split_axis=0, concat_axis=0, tiled=True)

    ids = jnp.stack([pair_near[0], pair_far[0], stack_bins[0]])
    ids = lax.all_gather(ids, "narrow", axis=2, tiled=True)
    near_ids, far_ids = ids[0], ids[1]
    bin_ids = ids[2].reshape(-1)

    with jax.named_scope("cross_spectra"):
        pieces = []
        for s in range(steps):
            far = gathered[:, s].transpose(1, 2, 0, 3).reshape(block_rows, 2, share)
            near_rows = select_rows(near, near_ids[s])
            far_rows = select_rows(far, far_ids[s])
            pieces.append(cross_rows(near_rows, far_rows, gain))
        cross_part = jnp.concatenate(pieces, axis=0)

    with jax.named_scope("lag_product"):
        lag_matrix = lag_rows(first_freq, share, freqs, LAGS)
        lagged = jnp.dot(cross_part, lag_matrix, preferred_element_type=jnp.float32)

    with jax.named_scope("bin_sums"):
        bin_hits = (
            jnp.arange(total_bins, dtype=jnp.int32)[:, None] == bin_ids[None, :]
        ).astype(jnp.float32)
        binned = jnp.dot(bin_hits, lagged, precision=lax.Precision.HIGHEST)
        binned = binned.reshape(narrow_count, wide_count * GW, LAGS)
        owned = lax.all_to_all(binned, "narrow", split_axis=0, concat_axis=0, tiled=True)
        owned = jnp.sum(owned, axis=0).reshape(wide_count, GW, LAGS)
        owned = lax.all_to_all(owned, "wide", split_axis=0, concat_axis=0, tiled=True)
        stacked = jnp.sum(owned, axis=0)

    inv_root = 1.0 / freqs**0.5
    stack_scale = (GW / (steps * pair_near.shape[2])) ** 0.5
    return (stacked * (inv_root * stack_scale))[None]


def solution(mesh):
    in_specs = (
        P("wide", None, None),
        P(),
        P(),
        P("wide", None, "narrow"),
        P("wide", None, "narrow"),
        P("wide", None, "narrow"),
    )
    out_specs = P("narrow", "wide", None)
    return jax.shard_map(local, mesh=mesh, in_specs=in_specs, out_specs=out_specs, check_vma=False)
```

```python
import jax
import jax.numpy as jnp
from jax import lax
from jax.sharding import PartitionSpec as P

LAGS = 1024
GW = 8


def trig_pair(freq_values, lag_values, freqs):
    turns = freq_values[:, None] * lag_values[None, :] % (2 * freqs)
    phase = turns.astype(jnp.float32) * (jnp.pi / freqs)
    return (jnp.cos(phase), jnp.sin(phase))


def lag_halves(first_freq, row_count, freqs, lag_count):
    unit_size = 64
    lag_values = jnp.arange(lag_count // 2, dtype=jnp.int32) + 1
    coarse_freq = first_freq + jnp.arange(row_count // unit_size, dtype=jnp.int32) * unit_size
    fine_freq = jnp.arange(unit_size, dtype=jnp.int32)
    coarse_cos, coarse_sin = trig_pair(coarse_freq, lag_values, freqs)
    fine_cos, fine_sin = trig_pair(fine_freq, lag_values, freqs)
    cosine = (
        coarse_cos[:, None, :] * fine_cos[None, :, :]
        - coarse_sin[:, None, :] * fine_sin[None, :, :]
    )
    sine = (
        coarse_sin[:, None, :] * fine_cos[None, :, :]
        + coarse_cos[:, None, :] * fine_sin[None, :, :]
    )
    cosine = cosine.reshape(row_count, lag_count // 2).astype(jnp.bfloat16)
    sine = sine.reshape(row_count, lag_count // 2).astype(jnp.bfloat16)
    return cosine, sine


def select_rows(block, indices):
    block_rows = block.shape[0]
    flat_block = block.reshape(block_rows, -1)
    picker = (indices[:, None] == jnp.arange(block_rows, dtype=jnp.int32)[None, :]).astype(
        jnp.bfloat16
    )
    chosen = jnp.dot(picker, flat_block, preferred_element_type=jnp.bfloat16)
    return chosen.reshape(indices.shape[0], 2, -1)


def cross_rows(near_rows, far_rows, band_gain):
    near_real = near_rows[:, 0].astype(jnp.float32)
    near_imag = near_rows[:, 1].astype(jnp.float32)
    far_real = far_rows[:, 0].astype(jnp.float32)
    far_imag = far_rows[:, 1].astype(jnp.float32)
    real_part = (near_real * far_real + near_imag * far_imag) * band_gain
    imag_part = (near_imag * far_real - near_real * far_imag) * band_gain
    return jnp.concatenate([real_part, imag_part], axis=1).astype(jnp.bfloat16)


def local(spectra, band_gain, owners, pair_near, pair_far, stack_bins):
    narrow_count = lax.axis_size("narrow")
    wide_count = lax.axis_size("wide")
    narrow_index = lax.axis_index("narrow")
    block_rows, _, freqs = spectra.shape
    steps = owners.shape[0]
    share = freqs // narrow_count
    piece = share // wide_count
    total_bins = narrow_count * wide_count * GW
    first_freq = narrow_index * share

    near = lax.dynamic_slice_in_dim(spectra, first_freq, share, axis=2)
    gain = lax.dynamic_slice_in_dim(band_gain, first_freq, share, axis=0)

    with jax.named_scope("owner_share_exchange"):
        outgoing = near.reshape(block_rows, 2, wide_count, piece).transpose(2, 0, 1, 3)
        arrived = lax.all_to_all(outgoing, "wide", split_axis=0, concat_axis=0, tiled=True)
        chosen = jnp.stack(
            [lax.dynamic_index_in_dim(arrived, owners[s], 0, keepdims=False) for s in range(steps)]
        )
        copies = jnp.broadcast_to(chosen[None], (wide_count,) + chosen.shape)
        gathered = lax.all_to_all(copies, "wide", split_axis=0, concat_axis=0, tiled=True)

    ids = jnp.stack([pair_near[0], pair_far[0], stack_bins[0]])
    ids = lax.all_gather(ids, "narrow", axis=2, tiled=True)
    near_ids, far_ids = ids[0], ids[1]
    bin_ids = ids[2].reshape(-1)

    with jax.named_scope("cross_spectra"):
        pieces = []
        for s in range(steps):
            far = gathered[:, s].transpose(1, 2, 0, 3).reshape(block_rows, 2, share)
            near_rows = select_rows(near, near_ids[s])
            far_rows = select_rows(far, far_ids[s])
            pieces.append(cross_rows(near_rows, far_rows, gain))
        cross_part = jnp.concatenate(pieces, axis=0)

    with jax.named_scope("bin_sums"):
        bin_hits = (
            jnp.arange(total_bins, dtype=jnp.int32)[:, None] == bin_ids[None, :]
        ).astype(jnp.bfloat16)
        bin_cross = jnp.dot(bin_hits, cross_part, preferred_element_type=jnp.float32)
        high = lax.reduce_precision(bin_cross, exponent_bits=8, mantissa_bits=7)
        low = bin_cross - high
        split = jnp.concatenate([high, low], axis=0).astype(jnp.bfloat16)

    with jax.named_scope("lag_product"):
        cosine, sine = lag_halves(first_freq, share, freqs, LAGS)
        even = jnp.dot(split[:, :share], cosine, preferred_element_type=jnp.float32)
        odd = jnp.dot(split[:, share:], sine, preferred_element_type=jnp.float32)
        even = even[:total_bins] + even[total_bins:]
        odd = odd[:total_bins] + odd[total_bins:]
        zero_lag = jnp.sum(bin_cross[:, :share], axis=1, keepdims=True)
        binned = jnp.concatenate(
            [jnp.flip(even + odd, axis=1), zero_lag, (even - odd)[:, : LAGS // 2 - 1]], axis=1
        )

    with jax.named_scope("bin_exchange"):
        binned = binned.reshape(narrow_count, wide_count * GW, LAGS)
        owned = lax.all_to_all(binned, "narrow", split_axis=0, concat_axis=0, tiled=True)
        owned = jnp.sum(owned, axis=0).reshape(wide_count, GW, LAGS)
        owned = lax.all_to_all(owned, "wide", split_axis=0, concat_axis=0, tiled=True)
        stacked = jnp.sum(owned, axis=0)

    inv_root = 1.0 / freqs**0.5
    stack_scale = (GW / (steps * pair_near.shape[2])) ** 0.5
    return (stacked * (inv_root * stack_scale))[None]


def solution(mesh):
    in_specs = (
        P("wide", None, None),
        P(),
        P(),
        P("wide", None, "narrow"),
        P("wide", None, "narrow"),
        P("wide", None, "narrow"),
    )
    out_specs = P("narrow", "wide", None)
    return jax.shard_map(local, mesh=mesh, in_specs=in_specs, out_specs=out_specs, check_vma=False)
```

```python
import jax
import jax.numpy as jnp
from jax import lax
from jax.sharding import PartitionSpec as P

LAGS = 1024
GW = 8


def trig_pair(freq_values, lag_values, freqs):
    turns = freq_values[:, None] * lag_values[None, :] % (2 * freqs)
    phase = turns.astype(jnp.float32) * (jnp.pi / freqs)
    return (jnp.cos(phase), jnp.sin(phase))


def lag_halves(first_freq, row_count, freqs, lag_count):
    unit_size = 64
    lag_values = jnp.arange(lag_count // 2, dtype=jnp.int32) + 1
    coarse_freq = first_freq + jnp.arange(row_count // unit_size, dtype=jnp.int32) * unit_size
    fine_freq = jnp.arange(unit_size, dtype=jnp.int32)
    coarse_cos, coarse_sin = trig_pair(coarse_freq, lag_values, freqs)
    fine_cos, fine_sin = trig_pair(fine_freq, lag_values, freqs)
    cosine = (
        coarse_cos[:, None, :] * fine_cos[None, :, :]
        - coarse_sin[:, None, :] * fine_sin[None, :, :]
    )
    sine = (
        coarse_sin[:, None, :] * fine_cos[None, :, :]
        + coarse_cos[:, None, :] * fine_sin[None, :, :]
    )
    cosine = cosine.reshape(row_count, lag_count // 2).astype(jnp.bfloat16)
    sine = sine.reshape(row_count, lag_count // 2).astype(jnp.bfloat16)
    return cosine, sine


def select_rows(block, indices):
    block_rows = block.shape[0]
    flat_block = block.reshape(block_rows, -1)
    picker = (indices[:, None] == jnp.arange(block_rows, dtype=jnp.int32)[None, :]).astype(
        jnp.bfloat16
    )
    chosen = jnp.dot(picker, flat_block, preferred_element_type=jnp.bfloat16)
    return chosen.reshape(indices.shape[0], 2, -1)


def cross_rows(near_rows, far_rows, band_gain):
    near_real = near_rows[:, 0].astype(jnp.float32)
    near_imag = near_rows[:, 1].astype(jnp.float32)
    far_real = far_rows[:, 0].astype(jnp.float32)
    far_imag = far_rows[:, 1].astype(jnp.float32)
    real_part = (near_real * far_real + near_imag * far_imag) * band_gain
    imag_part = (near_imag * far_real - near_real * far_imag) * band_gain
    return jnp.concatenate([real_part, imag_part], axis=1).astype(jnp.bfloat16)


def local(spectra, band_gain, owners, pair_near, pair_far, stack_bins):
    narrow_count = lax.axis_size("narrow")
    wide_count = lax.axis_size("wide")
    narrow_index = lax.axis_index("narrow")
    block_rows, _, freqs = spectra.shape
    steps = owners.shape[0]
    share = freqs // narrow_count
    piece = share // wide_count
    total_bins = narrow_count * wide_count * GW
    first_freq = narrow_index * share

    near = lax.dynamic_slice_in_dim(spectra, first_freq, share, axis=2)
    gain = lax.dynamic_slice_in_dim(band_gain, first_freq, share, axis=0)

    with jax.named_scope("owner_share_exchange"):
        outgoing = near.reshape(block_rows, 2, wide_count, piece).transpose(2, 0, 1, 3)
        arrived = lax.all_to_all(outgoing, "wide", split_axis=0, concat_axis=0, tiled=True)
        chosen = jnp.stack(
            [lax.dynamic_index_in_dim(arrived, owners[s], 0, keepdims=False) for s in range(steps)]
        )
        copies = jnp.broadcast_to(chosen[None], (wide_count,) + chosen.shape)
        gathered = lax.all_to_all(copies, "wide", split_axis=0, concat_axis=0, tiled=True)

    ids = jnp.stack([pair_near[0], pair_far[0], stack_bins[0]])
    ids = lax.all_gather(ids, "narrow", axis=2, tiled=True)
    near_ids, far_ids = ids[0], ids[1]
    bin_ids = ids[2].reshape(-1)

    with jax.named_scope("cross_spectra"):
        pieces = []
        for s in range(steps):
            far = gathered[:, s].transpose(1, 2, 0, 3).reshape(block_rows, 2, share)
            near_rows = select_rows(near, near_ids[s])
            far_rows = select_rows(far, far_ids[s])
            pieces.append(cross_rows(near_rows, far_rows, gain))
        cross_part = lax.optimization_barrier(jnp.concatenate(pieces, axis=0))

    with jax.named_scope("bin_sums"):
        bin_hits = (
            jnp.arange(total_bins, dtype=jnp.int32)[:, None] == bin_ids[None, :]
        ).astype(jnp.bfloat16)
        bin_cross = jnp.dot(bin_hits, cross_part, preferred_element_type=jnp.float32)
        high = lax.reduce_precision(bin_cross, exponent_bits=8, mantissa_bits=7)
        low = bin_cross - high
        split = jnp.concatenate([high, low], axis=0).astype(jnp.bfloat16)

    with jax.named_scope("lag_product"):
        cosine, sine = lag_halves(first_freq, share, freqs, LAGS)
        even = jnp.dot(split[:, :share], cosine, preferred_element_type=jnp.float32)
        odd = jnp.dot(split[:, share:], sine, preferred_element_type=jnp.float32)
        even = even[:total_bins] + even[total_bins:]
        odd = odd[:total_bins] + odd[total_bins:]
        zero_lag = jnp.sum(bin_cross[:, :share], axis=1, keepdims=True)
        binned = jnp.concatenate(
            [even + odd, zero_lag, (even - odd)[:, : LAGS // 2 - 1]], axis=1
        )

    with jax.named_scope("bin_exchange"):
        binned = binned.reshape(narrow_count, wide_count * GW, LAGS)
        owned = lax.all_to_all(binned, "narrow", split_axis=0, concat_axis=0, tiled=True)
        owned = jnp.sum(owned, axis=0).reshape(wide_count, GW, LAGS)
        owned = lax.all_to_all(owned, "wide", split_axis=0, concat_axis=0, tiled=True)
        stacked = jnp.sum(owned, axis=0)
        stacked = jnp.concatenate(
            [jnp.flip(stacked[:, : LAGS // 2], axis=1), stacked[:, LAGS // 2 :]], axis=1
        )

    inv_root = 1.0 / freqs**0.5
    stack_scale = (GW / (steps * pair_near.shape[2])) ** 0.5
    return (stacked * (inv_root * stack_scale))[None]


def solution(mesh):
    in_specs = (
        P("wide", None, None),
        P(),
        P(),
        P("wide", None, "narrow"),
        P("wide", None, "narrow"),
        P("wide", None, "narrow"),
    )
    out_specs = P("narrow", "wide", None)
    return jax.shard_map(local, mesh=mesh, in_specs=in_specs, out_specs=out_specs, check_vma=False)
```

```python
import jax
import jax.numpy as jnp
from jax import lax
from jax.sharding import PartitionSpec as P

LAGS = 1024
GW = 8


def trig_pair(freq_values, lag_values, freqs):
    turns = freq_values[:, None] * lag_values[None, :] % (2 * freqs)
    phase = turns.astype(jnp.float32) * (jnp.pi / freqs)
    return (jnp.cos(phase), jnp.sin(phase))


def lag_halves(first_freq, row_count, freqs, lag_count):
    unit_size = 64
    lag_values = jnp.arange(lag_count // 2, dtype=jnp.int32) + 1
    coarse_freq = first_freq + jnp.arange(row_count // unit_size, dtype=jnp.int32) * unit_size
    fine_freq = jnp.arange(unit_size, dtype=jnp.int32)
    coarse_cos, coarse_sin = trig_pair(coarse_freq, lag_values, freqs)
    fine_cos, fine_sin = trig_pair(fine_freq, lag_values, freqs)
    cosine = (
        coarse_cos[:, None, :] * fine_cos[None, :, :]
        - coarse_sin[:, None, :] * fine_sin[None, :, :]
    )
    sine = (
        coarse_sin[:, None, :] * fine_cos[None, :, :]
        + coarse_cos[:, None, :] * fine_sin[None, :, :]
    )
    cosine = cosine.reshape(row_count, lag_count // 2).astype(jnp.bfloat16)
    sine = sine.reshape(row_count, lag_count // 2).astype(jnp.bfloat16)
    return cosine, sine


def select_rows(block, indices):
    block_rows = block.shape[0]
    flat_block = block.reshape(block_rows, -1)
    picker = (indices[:, None] == jnp.arange(block_rows, dtype=jnp.int32)[None, :]).astype(
        jnp.bfloat16
    )
    chosen = jnp.dot(picker, flat_block, preferred_element_type=jnp.bfloat16)
    return chosen.reshape(indices.shape[0], 2, -1)


def cross_rows(near_rows, far_rows, band_gain):
    near_real = near_rows[:, 0].astype(jnp.float32)
    near_imag = near_rows[:, 1].astype(jnp.float32)
    far_real = far_rows[:, 0].astype(jnp.float32)
    far_imag = far_rows[:, 1].astype(jnp.float32)
    real_part = (near_real * far_real + near_imag * far_imag) * band_gain
    imag_part = (near_imag * far_real - near_real * far_imag) * band_gain
    return real_part.astype(jnp.bfloat16), imag_part.astype(jnp.bfloat16)


def split_product(values, table):
    high = lax.reduce_precision(values, exponent_bits=8, mantissa_bits=7)
    low = values - high
    return jnp.dot(
        high.astype(jnp.bfloat16), table, preferred_element_type=jnp.float32
    ) + jnp.dot(low.astype(jnp.bfloat16), table, preferred_element_type=jnp.float32)


def local(spectra, band_gain, owners, pair_near, pair_far, stack_bins):
    narrow_count = lax.axis_size("narrow")
    wide_count = lax.axis_size("wide")
    narrow_index = lax.axis_index("narrow")
    block_rows, _, freqs = spectra.shape
    steps = owners.shape[0]
    share = freqs // narrow_count
    piece = share // wide_count
    total_bins = narrow_count * wide_count * GW
    first_freq = narrow_index * share

    near = lax.dynamic_slice_in_dim(spectra, first_freq, share, axis=2)
    gain = lax.dynamic_slice_in_dim(band_gain, first_freq, share, axis=0)

    with jax.named_scope("owner_share_exchange"):
        outgoing = near.reshape(block_rows, 2, wide_count, piece).transpose(2, 0, 1, 3)
        arrived = lax.all_to_all(outgoing, "wide", split_axis=0, concat_axis=0, tiled=True)
        chosen = jnp.stack(
            [lax.dynamic_index_in_dim(arrived, owners[s], 0, keepdims=False) for s in range(steps)]
        )
        copies = jnp.broadcast_to(chosen[None], (wide_count,) + chosen.shape)
        gathered = lax.all_to_all(copies, "wide", split_axis=0, concat_axis=0, tiled=True)

    ids = jnp.stack([pair_near[0], pair_far[0], stack_bins[0]])
    ids = lax.all_gather(ids, "narrow", axis=2, tiled=True)
    near_ids, far_ids = ids[0], ids[1]
    bin_ids = ids[2]

    with jax.named_scope("cross_spectra"):
        parts = []
        for s in range(steps):
            far = gathered[:, s].transpose(1, 2, 0, 3).reshape(block_rows, 2, share)
            near_rows = select_rows(near, near_ids[s])
            far_rows = select_rows(far, far_ids[s])
            parts.append(lax.optimization_barrier(cross_rows(near_rows, far_rows, gain)))

    with jax.named_scope("bin_sums"):
        real_sum = None
        imag_sum = None
        for s in range(steps):
            bin_hits = (
                jnp.arange(total_bins, dtype=jnp.int32)[:, None] == bin_ids[s][None, :]
            ).astype(jnp.bfloat16)
            real_step = jnp.dot(bin_hits, parts[s][0], preferred_element_type=jnp.float32)
            imag_step = jnp.dot(bin_hits, parts[s][1], preferred_element_type=jnp.float32)
            real_sum = real_step if real_sum is None else real_sum + real_step
            imag_sum = imag_step if imag_sum is None else imag_sum + imag_step

    with jax.named_scope("lag_product"):
        cosine, sine = lag_halves(first_freq, share, freqs, LAGS)
        even = split_product(real_sum, cosine)
        odd = split_product(imag_sum, sine)
        zero_lag = jnp.sum(real_sum, axis=1, keepdims=True)
        last = jnp.arange(LAGS // 2, dtype=jnp.int32)[None, :] == LAGS // 2 - 1
        binned = jnp.stack([even + odd, jnp.where(last, zero_lag, even - odd)])

    with jax.named_scope("bin_exchange"):
        binned = binned.reshape(2, narrow_count, wide_count * GW, LAGS // 2)
        owned = lax.all_to_all(binned, "narrow", split_axis=1, concat_axis=1, tiled=True)
        owned = jnp.sum(owned, axis=1).reshape(2, wide_count, GW, LAGS // 2)
        owned = lax.all_to_all(owned, "wide", split_axis=1, concat_axis=1, tiled=True)
        plus, minus = jnp.sum(owned, axis=1)
        stacked = jnp.concatenate(
            [jnp.flip(plus, axis=1), minus[:, LAGS // 2 - 1 :], minus[:, : LAGS // 2 - 1]], axis=1
        )

    inv_root = 1.0 / freqs**0.5
    stack_scale = (GW / (steps * pair_near.shape[2])) ** 0.5
    return (stacked * (inv_root * stack_scale))[None]


def solution(mesh):
    in_specs = (
        P("wide", None, None),
        P(),
        P(),
        P("wide", None, "narrow"),
        P("wide", None, "narrow"),
        P("wide", None, "narrow"),
    )
    out_specs = P("narrow", "wide", None)
    return jax.shard_map(local, mesh=mesh, in_specs=in_specs, out_specs=out_specs, check_vma=False)
```

```python
import jax
import jax.numpy as jnp
from jax import lax
from jax.sharding import PartitionSpec as P

LAGS = 1024
GW = 8


def trig_pair(freq_values, lag_values, freqs):
    turns = freq_values[:, None] * lag_values[None, :] % (2 * freqs)
    phase = turns.astype(jnp.float32) * (jnp.pi / freqs)
    return (jnp.cos(phase), jnp.sin(phase))


def lag_halves(first_freq, row_count, freqs, lag_count):
    unit_size = 64
    lag_values = jnp.arange(lag_count // 2, dtype=jnp.int32) + 1
    coarse_freq = first_freq + jnp.arange(row_count // unit_size, dtype=jnp.int32) * unit_size
    fine_freq = jnp.arange(unit_size, dtype=jnp.int32)
    coarse_cos, coarse_sin = trig_pair(coarse_freq, lag_values, freqs)
    fine_cos, fine_sin = trig_pair(fine_freq, lag_values, freqs)
    cosine = (
        coarse_cos[:, None, :] * fine_cos[None, :, :]
        - coarse_sin[:, None, :] * fine_sin[None, :, :]
    )
    sine = (
        coarse_sin[:, None, :] * fine_cos[None, :, :]
        + coarse_cos[:, None, :] * fine_sin[None, :, :]
    )
    cosine = cosine.reshape(row_count, lag_count // 2).astype(jnp.bfloat16)
    sine = sine.reshape(row_count, lag_count // 2).astype(jnp.bfloat16)
    return cosine, sine


def select_rows(block, indices):
    block_rows = block.shape[0]
    flat_block = block.reshape(block_rows, -1)
    picker = (indices[:, None] == jnp.arange(block_rows, dtype=jnp.int32)[None, :]).astype(
        jnp.bfloat16
    )
    chosen = jnp.dot(picker, flat_block, preferred_element_type=jnp.bfloat16)
    return chosen.reshape(indices.shape[0], 2, -1)


def cross_rows(near_rows, far_rows, band_gain):
    near_real = near_rows[:, 0].astype(jnp.float32)
    near_imag = near_rows[:, 1].astype(jnp.float32)
    far_real = far_rows[:, 0].astype(jnp.float32)
    far_imag = far_rows[:, 1].astype(jnp.float32)
    real_part = (near_real * far_real + near_imag * far_imag) * band_gain
    imag_part = (near_imag * far_real - near_real * far_imag) * band_gain
    return real_part.astype(jnp.bfloat16), imag_part.astype(jnp.bfloat16)


def split_product(values, table):
    high = lax.reduce_precision(values, exponent_bits=8, mantissa_bits=7)
    low = values - high
    return jnp.dot(
        high.astype(jnp.bfloat16), table, preferred_element_type=jnp.float32
    ) + jnp.dot(low.astype(jnp.bfloat16), table, preferred_element_type=jnp.float32)


def local(spectra, band_gain, owners, pair_near, pair_far, stack_bins):
    narrow_count = lax.axis_size("narrow")
    wide_count = lax.axis_size("wide")
    narrow_index = lax.axis_index("narrow")
    block_rows, _, freqs = spectra.shape
    steps = owners.shape[0]
    share = freqs // narrow_count
    piece = share // wide_count
    total_bins = narrow_count * wide_count * GW
    first_freq = narrow_index * share

    near = lax.dynamic_slice_in_dim(spectra, first_freq, share, axis=2)
    gain = lax.dynamic_slice_in_dim(band_gain, first_freq, share, axis=0)

    with jax.named_scope("owner_share_exchange"):
        outgoing = near.reshape(block_rows, 2, wide_count, piece)
        arrived = lax.all_to_all(outgoing, "wide", split_axis=2, concat_axis=2, tiled=True)
        gathered = []
        for s in range(steps):
            chosen = lax.dynamic_index_in_dim(arrived, owners[s], 2, keepdims=False)
            copies = jnp.broadcast_to(chosen[None], (wide_count,) + chosen.shape)
            gathered.append(lax.all_to_all(copies, "wide", split_axis=0, concat_axis=0, tiled=True))

    ids = jnp.stack([pair_near[0], pair_far[0], stack_bins[0]]).astype(jnp.float32)
    ids = lax.all_gather(ids, "narrow", axis=2, tiled=True).astype(jnp.int32)
    near_ids, far_ids = ids[0], ids[1]
    bin_ids = ids[2]

    with jax.named_scope("cross_spectra"):
        parts = []
        for s in range(steps):
            far = gathered[s].transpose(1, 2, 0, 3).reshape(block_rows, 2, share)
            near_rows = select_rows(near, near_ids[s])
            far_rows = select_rows(far, far_ids[s])
            parts.append(lax.optimization_barrier(cross_rows(near_rows, far_rows, gain)))

    with jax.named_scope("bin_sums"):
        real_sum = None
        imag_sum = None
        for s in range(steps):
            bin_hits = (
                jnp.arange(total_bins, dtype=jnp.int32)[:, None] == bin_ids[s][None, :]
            ).astype(jnp.bfloat16)
            real_step = jnp.dot(bin_hits, parts[s][0], preferred_element_type=jnp.float32)
            imag_step = jnp.dot(bin_hits, parts[s][1], preferred_element_type=jnp.float32)
            real_sum = real_step if real_sum is None else real_sum + real_step
            imag_sum = imag_step if imag_sum is None else imag_sum + imag_step

    with jax.named_scope("lag_product"):
        cosine, sine = lag_halves(first_freq, share, freqs, LAGS)
        even = split_product(real_sum, cosine)
        odd = split_product(imag_sum, sine)
        zero_lag = jnp.sum(real_sum, axis=1, keepdims=True)
        last = jnp.arange(LAGS // 2, dtype=jnp.int32)[None, :] == LAGS // 2 - 1
        binned = jnp.stack([even + odd, jnp.where(last, zero_lag, even - odd)])

    with jax.named_scope("bin_exchange"):
        binned = binned.reshape(2, narrow_count, wide_count * GW, LAGS // 2)
        owned = lax.all_to_all(binned, "narrow", split_axis=1, concat_axis=1, tiled=True)
        owned = jnp.sum(owned, axis=1).reshape(2, wide_count, GW, LAGS // 2)
        owned = lax.all_to_all(owned, "wide", split_axis=1, concat_axis=1, tiled=True)
        plus, minus = jnp.sum(owned, axis=1)
        stacked = jnp.concatenate(
            [jnp.flip(plus, axis=1), minus[:, LAGS // 2 - 1 :], minus[:, : LAGS // 2 - 1]], axis=1
        )

    inv_root = 1.0 / freqs**0.5
    stack_scale = (GW / (steps * pair_near.shape[2])) ** 0.5
    return (stacked * (inv_root * stack_scale))[None]


def solution(mesh):
    in_specs = (
        P("wide", None, None),
        P(),
        P(),
        P("wide", None, "narrow"),
        P("wide", None, "narrow"),
        P("wide", None, "narrow"),
    )
    out_specs = P("narrow", "wide", None)
    return jax.shard_map(local, mesh=mesh, in_specs=in_specs, out_specs=out_specs, check_vma=False)
```

```python
import jax
import jax.numpy as jnp
from jax import lax
from jax.sharding import PartitionSpec as P

LAGS = 1024
GW = 8


def trig_pair(freq_values, lag_values, freqs):
    turns = freq_values[:, None] * lag_values[None, :] % (2 * freqs)
    phase = turns.astype(jnp.float32) * (jnp.pi / freqs)
    return (jnp.cos(phase), jnp.sin(phase))


def lag_halves(first_freq, row_count, freqs, lag_count):
    unit_size = 64
    lag_values = jnp.arange(lag_count // 2, dtype=jnp.int32) + 1
    coarse_freq = first_freq + jnp.arange(row_count // unit_size, dtype=jnp.int32) * unit_size
    fine_freq = jnp.arange(unit_size, dtype=jnp.int32)
    coarse_cos, coarse_sin = trig_pair(coarse_freq, lag_values, freqs)
    fine_cos, fine_sin = trig_pair(fine_freq, lag_values, freqs)
    cosine = (
        coarse_cos[:, None, :] * fine_cos[None, :, :]
        - coarse_sin[:, None, :] * fine_sin[None, :, :]
    )
    sine = (
        coarse_sin[:, None, :] * fine_cos[None, :, :]
        + coarse_cos[:, None, :] * fine_sin[None, :, :]
    )
    cosine = cosine.reshape(row_count, lag_count // 2).astype(jnp.bfloat16)
    sine = sine.reshape(row_count, lag_count // 2).astype(jnp.bfloat16)
    return cosine, sine


def select_rows(block, indices):
    block_rows = block.shape[0]
    flat_block = block.reshape(block_rows, -1)
    picker = (indices[:, None] == jnp.arange(block_rows, dtype=jnp.int32)[None, :]).astype(
        jnp.bfloat16
    )
    chosen = jnp.dot(picker, flat_block, preferred_element_type=jnp.bfloat16)
    return chosen.reshape(indices.shape[0], 2, -1)


def cross_rows(near_rows, far_rows, band_gain):
    near_real = near_rows[:, 0].astype(jnp.float32)
    near_imag = near_rows[:, 1].astype(jnp.float32)
    far_real = far_rows[:, 0].astype(jnp.float32)
    far_imag = far_rows[:, 1].astype(jnp.float32)
    real_part = (near_real * far_real + near_imag * far_imag) * band_gain
    imag_part = (near_imag * far_real - near_real * far_imag) * band_gain
    return real_part.astype(jnp.bfloat16), imag_part.astype(jnp.bfloat16)


def split_product(values, table):
    high = lax.reduce_precision(values, exponent_bits=8, mantissa_bits=7)
    low = values - high
    return jnp.dot(
        high.astype(jnp.bfloat16), table, preferred_element_type=jnp.float32
    ) + jnp.dot(low.astype(jnp.bfloat16), table, preferred_element_type=jnp.float32)


def halving_sum(parts, axis, count):
    index = lax.axis_index(axis)
    bit = 1
    while bit < count:
        mine = (index // bit) % 2
        paired = parts.reshape((parts.shape[0], parts.shape[1] // 2, 2) + parts.shape[2:])
        first, second = paired[:, :, 0], paired[:, :, 1]
        keep = jnp.where(mine == 0, first, second)
        send = jnp.where(mine == 0, second, first)
        pairs = [(i, i ^ bit) for i in range(count)]
        parts = keep + lax.ppermute(send, axis, pairs)
        bit *= 2
    return parts[:, 0]


def local(spectra, band_gain, owners, pair_near, pair_far, stack_bins):
    narrow_count = lax.axis_size("narrow")
    wide_count = lax.axis_size("wide")
    narrow_index = lax.axis_index("narrow")
    block_rows, _, freqs = spectra.shape
    steps = owners.shape[0]
    share = freqs // narrow_count
    piece = share // wide_count
    total_bins = narrow_count * wide_count * GW
    first_freq = narrow_index * share

    near = lax.dynamic_slice_in_dim(spectra, first_freq, share, axis=2)
    gain = lax.dynamic_slice_in_dim(band_gain, first_freq, share, axis=0)

    with jax.named_scope("owner_share_exchange"):
        outgoing = near.reshape(block_rows, 2, wide_count, piece).transpose(2, 0, 1, 3)
        arrived = lax.all_to_all(outgoing, "wide", split_axis=0, concat_axis=0, tiled=True)
        chosen = jnp.stack(
            [lax.dynamic_index_in_dim(arrived, owners[s], 0, keepdims=False) for s in range(steps)]
        )
        copies = jnp.broadcast_to(chosen[None], (wide_count,) + chosen.shape)
        gathered = lax.all_to_all(copies, "wide", split_axis=0, concat_axis=0, tiled=True)

    ids = jnp.stack([pair_near[0], pair_far[0], stack_bins[0]])
    ids = lax.all_gather(ids, "narrow", axis=2, tiled=True)
    near_ids, far_ids = ids[0], ids[1]
    bin_ids = ids[2]

    with jax.named_scope("cross_spectra"):
        parts = []
        for s in range(steps):
            far = gathered[:, s].transpose(1, 2, 0, 3).reshape(block_rows, 2, share)
            near_rows = select_rows(near, near_ids[s])
            far_rows = select_rows(far, far_ids[s])
            parts.append(lax.optimization_barrier(cross_rows(near_rows, far_rows, gain)))

    with jax.named_scope("bin_sums"):
        real_sum = None
        imag_sum = None
        for s in range(steps):
            bin_hits = (
                jnp.arange(total_bins, dtype=jnp.int32)[:, None] == bin_ids[s][None, :]
            ).astype(jnp.bfloat16)
            real_step = jnp.dot(bin_hits, parts[s][0], preferred_element_type=jnp.float32)
            imag_step = jnp.dot(bin_hits, parts[s][1], preferred_element_type=jnp.float32)
            real_sum = real_step if real_sum is None else real_sum + real_step
            imag_sum = imag_step if imag_sum is None else imag_sum + imag_step

    with jax.named_scope("lag_product"):
        cosine, sine = lag_halves(first_freq, share, freqs, LAGS)
        even = split_product(real_sum, cosine)
        odd = split_product(imag_sum, sine)
        zero_lag = jnp.sum(real_sum, axis=1, keepdims=True)
        last = jnp.arange(LAGS // 2, dtype=jnp.int32)[None, :] == LAGS // 2 - 1
        binned = jnp.stack([even + odd, jnp.where(last, zero_lag, even - odd)])

    with jax.named_scope("bin_exchange"):
        binned = binned.reshape(2, narrow_count, wide_count * GW, LAGS // 2)
        owned = halving_sum(binned, "narrow", narrow_count)
        owned = owned.reshape(2, wide_count, GW, LAGS // 2)
        owned = lax.all_to_all(owned, "wide", split_axis=1, concat_axis=1, tiled=True)
        plus, minus = jnp.sum(owned, axis=1)
        stacked = jnp.concatenate(
            [jnp.flip(plus, axis=1), minus[:, LAGS // 2 - 1 :], minus[:, : LAGS // 2 - 1]], axis=1
        )

    inv_root = 1.0 / freqs**0.5
    stack_scale = (GW / (steps * pair_near.shape[2])) ** 0.5
    return (stacked * (inv_root * stack_scale))[None]


def solution(mesh):
    in_specs = (
        P("wide", None, None),
        P(),
        P(),
        P("wide", None, "narrow"),
        P("wide", None, "narrow"),
        P("wide", None, "narrow"),
    )
    out_specs = P("narrow", "wide", None)
    return jax.shard_map(local, mesh=mesh, in_specs=in_specs, out_specs=out_specs, check_vma=False)
```

```python
import jax
import jax.numpy as jnp
from jax import lax
from jax.sharding import PartitionSpec as P

LAGS = 1024
GW = 8


def trig_pair(freq_values, lag_values, freqs):
    turns = freq_values[:, None] * lag_values[None, :] % (2 * freqs)
    phase = turns.astype(jnp.float32) * (jnp.pi / freqs)
    return (jnp.cos(phase), jnp.sin(phase))


def lag_halves(first_freq, row_count, freqs, lag_count):
    unit_size = 64
    lag_values = jnp.arange(lag_count // 2, dtype=jnp.int32) + 1
    coarse_freq = first_freq + jnp.arange(row_count // unit_size, dtype=jnp.int32) * unit_size
    fine_freq = jnp.arange(unit_size, dtype=jnp.int32)
    coarse_cos, coarse_sin = trig_pair(coarse_freq, lag_values, freqs)
    fine_cos, fine_sin = trig_pair(fine_freq, lag_values, freqs)
    cosine = (
        coarse_cos[:, None, :] * fine_cos[None, :, :]
        - coarse_sin[:, None, :] * fine_sin[None, :, :]
    )
    sine = (
        coarse_sin[:, None, :] * fine_cos[None, :, :]
        + coarse_cos[:, None, :] * fine_sin[None, :, :]
    )
    cosine = cosine.reshape(row_count, lag_count // 2).astype(jnp.bfloat16)
    sine = sine.reshape(row_count, lag_count // 2).astype(jnp.bfloat16)
    return cosine, sine


def select_rows(block, indices):
    block_rows = block.shape[0]
    flat_block = block.reshape(block_rows, -1)
    picker = (indices[:, None] == jnp.arange(block_rows, dtype=jnp.int32)[None, :]).astype(
        jnp.bfloat16
    )
    chosen = jnp.dot(picker, flat_block, preferred_element_type=jnp.bfloat16)
    return chosen.reshape(indices.shape[0], 2, -1)


def cross_rows(near_rows, far_rows, band_gain):
    near_real = near_rows[:, 0].astype(jnp.float32)
    near_imag = near_rows[:, 1].astype(jnp.float32)
    far_real = far_rows[:, 0].astype(jnp.float32)
    far_imag = far_rows[:, 1].astype(jnp.float32)
    real_part = (near_real * far_real + near_imag * far_imag) * band_gain
    imag_part = (near_imag * far_real - near_real * far_imag) * band_gain
    return real_part.astype(jnp.bfloat16), imag_part.astype(jnp.bfloat16)


def split_product(values, table):
    high = lax.reduce_precision(values, exponent_bits=8, mantissa_bits=7)
    low = values - high
    return jnp.dot(
        high.astype(jnp.bfloat16), table, preferred_element_type=jnp.float32
    ) + jnp.dot(low.astype(jnp.bfloat16), table, preferred_element_type=jnp.float32)


def halving_sum(parts, axis, count):
    index = lax.axis_index(axis)
    bit = 1
    while bit < count:
        mine = (index // bit) % 2
        paired = parts.reshape((parts.shape[0], parts.shape[1] // 2, 2) + parts.shape[2:])
        first, second = paired[:, :, 0], paired[:, :, 1]
        keep = jnp.where(mine == 0, first, second)
        send = jnp.where(mine == 0, second, first)
        pairs = [(i, i ^ bit) for i in range(count)]
        parts = keep + lax.ppermute(send, axis, pairs)
        bit *= 2
    return parts[:, 0]


def local(spectra, band_gain, owners, pair_near, pair_far, stack_bins):
    narrow_count = lax.axis_size("narrow")
    wide_count = lax.axis_size("wide")
    narrow_index = lax.axis_index("narrow")
    block_rows, _, freqs = spectra.shape
    steps = owners.shape[0]
    share = freqs // narrow_count
    piece = share // wide_count
    total_bins = narrow_count * wide_count * GW
    first_freq = narrow_index * share

    near = lax.dynamic_slice_in_dim(spectra, first_freq, share, axis=2)
    gain = lax.dynamic_slice_in_dim(band_gain, first_freq, share, axis=0)

    with jax.named_scope("owner_share_exchange"):
        outgoing = near.reshape(block_rows, 2, wide_count, piece).transpose(2, 0, 1, 3)
        arrived = lax.all_to_all(outgoing, "wide", split_axis=0, concat_axis=0, tiled=True)
        chosen = jnp.stack(
            [lax.dynamic_index_in_dim(arrived, owners[s], 0, keepdims=False) for s in range(steps)]
        )
        copies = jnp.broadcast_to(chosen[None], (wide_count,) + chosen.shape)
        gathered = lax.all_to_all(copies, "wide", split_axis=0, concat_axis=0, tiled=True)

    ids = jnp.stack([pair_near[0], pair_far[0], stack_bins[0]])
    ids = lax.all_gather(ids, "narrow", axis=2, tiled=True)
    near_ids, far_ids = ids[0], ids[1]
    bin_ids = ids[2]

    with jax.named_scope("cross_spectra"):
        parts = []
        for s in range(steps):
            far = gathered[:, s].transpose(1, 2, 0, 3).reshape(block_rows, 2, share)
            near_rows = select_rows(near, near_ids[s])
            far_rows = select_rows(far, far_ids[s])
            parts.append(lax.optimization_barrier(cross_rows(near_rows, far_rows, gain)))

    with jax.named_scope("bin_sums"):
        real_sum = None
        imag_sum = None
        for s in range(steps):
            bin_hits = (
                jnp.arange(total_bins, dtype=jnp.int32)[:, None] == bin_ids[s][None, :]
            ).astype(jnp.bfloat16)
            real_step = jnp.dot(bin_hits, parts[s][0], preferred_element_type=jnp.float32)
            imag_step = jnp.dot(bin_hits, parts[s][1], preferred_element_type=jnp.float32)
            real_sum = real_step if real_sum is None else real_sum + real_step
            imag_sum = imag_step if imag_sum is None else imag_sum + imag_step

    with jax.named_scope("lag_product"):
        cosine, sine = lag_halves(first_freq, share, freqs, LAGS)
        even = split_product(real_sum, cosine)
        odd = split_product(imag_sum, sine)
        zero_lag = jnp.sum(real_sum, axis=1, keepdims=True)
        last = jnp.arange(LAGS // 2, dtype=jnp.int32)[None, :] == LAGS // 2 - 1
        binned = jnp.stack([even + odd, jnp.where(last, zero_lag, even - odd)])

    with jax.named_scope("bin_exchange"):
        binned = binned.reshape(2, narrow_count, wide_count * GW, LAGS // 2)
        owned = halving_sum(binned, "narrow", narrow_count)
        owned = owned.reshape(2, wide_count, GW, LAGS // 2)
        plus, minus = halving_sum(owned, "wide", wide_count)
        stacked = jnp.concatenate(
            [jnp.flip(plus, axis=1), minus[:, LAGS // 2 - 1 :], minus[:, : LAGS // 2 - 1]], axis=1
        )

    inv_root = 1.0 / freqs**0.5
    stack_scale = (GW / (steps * pair_near.shape[2])) ** 0.5
    return (stacked * (inv_root * stack_scale))[None]


def solution(mesh):
    in_specs = (
        P("wide", None, None),
        P(),
        P(),
        P("wide", None, "narrow"),
        P("wide", None, "narrow"),
        P("wide", None, "narrow"),
    )
    out_specs = P("narrow", "wide", None)
    return jax.shard_map(local, mesh=mesh, in_specs=in_specs, out_specs=out_specs, check_vma=False)
```

```python
import jax
import jax.numpy as jnp
from jax import lax
from jax.sharding import PartitionSpec as P

LAGS = 1024
GW = 8


def trig_pair(freq_values, lag_values, freqs):
    turns = freq_values[:, None] * lag_values[None, :] % (2 * freqs)
    phase = turns.astype(jnp.float32) * (jnp.pi / freqs)
    return (jnp.cos(phase), jnp.sin(phase))


def lag_halves(first_freq, row_count, freqs, lag_count):
    unit_size = 64
    lag_values = jnp.arange(lag_count // 2, dtype=jnp.int32) + 1
    coarse_freq = first_freq + jnp.arange(row_count // unit_size, dtype=jnp.int32) * unit_size
    fine_freq = jnp.arange(unit_size, dtype=jnp.int32)
    coarse_cos, coarse_sin = trig_pair(coarse_freq, lag_values, freqs)
    fine_cos, fine_sin = trig_pair(fine_freq, lag_values, freqs)
    cosine = (
        coarse_cos[:, None, :] * fine_cos[None, :, :]
        - coarse_sin[:, None, :] * fine_sin[None, :, :]
    )
    sine = (
        coarse_sin[:, None, :] * fine_cos[None, :, :]
        + coarse_cos[:, None, :] * fine_sin[None, :, :]
    )
    cosine = cosine.reshape(row_count, lag_count // 2).astype(jnp.bfloat16)
    sine = sine.reshape(row_count, lag_count // 2).astype(jnp.bfloat16)
    return cosine, sine


def select_rows(block, indices):
    block_rows = block.shape[0]
    flat_block = block.reshape(block_rows, -1)
    picker = (indices[:, None] == jnp.arange(block_rows, dtype=jnp.int32)[None, :]).astype(
        jnp.bfloat16
    )
    chosen = jnp.dot(picker, flat_block, preferred_element_type=jnp.bfloat16)
    return chosen.reshape(indices.shape[0], 2, -1)


def cross_rows(near_rows, far_rows, band_gain):
    near_real = near_rows[:, 0].astype(jnp.float32)
    near_imag = near_rows[:, 1].astype(jnp.float32)
    far_real = far_rows[:, 0].astype(jnp.float32)
    far_imag = far_rows[:, 1].astype(jnp.float32)
    real_part = (near_real * far_real + near_imag * far_imag) * band_gain
    imag_part = (near_imag * far_real - near_real * far_imag) * band_gain
    return real_part.astype(jnp.bfloat16), imag_part.astype(jnp.bfloat16)


def split_product(values, table):
    high = lax.reduce_precision(values, exponent_bits=8, mantissa_bits=7)
    low = values - high
    split = jnp.concatenate([high, low], axis=0).astype(jnp.bfloat16)
    both = jnp.dot(split, table, preferred_element_type=jnp.float32)
    return both[: values.shape[0]] + both[values.shape[0] :]


def halving_sum(parts, axis, count):
    index = lax.axis_index(axis)
    bit = 1
    while bit < count:
        mine = (index // bit) % 2
        paired = parts.reshape((parts.shape[0], parts.shape[1] // 2, 2) + parts.shape[2:])
        first, second = paired[:, :, 0], paired[:, :, 1]
        keep = jnp.where(mine == 0, first, second)
        send = jnp.where(mine == 0, second, first)
        pairs = [(i, i ^ bit) for i in range(count)]
        parts = keep + lax.ppermute(send, axis, pairs)
        bit *= 2
    return parts[:, 0]


def local(spectra, band_gain, owners, pair_near, pair_far, stack_bins):
    narrow_count = lax.axis_size("narrow")
    wide_count = lax.axis_size("wide")
    narrow_index = lax.axis_index("narrow")
    block_rows, _, freqs = spectra.shape
    steps = owners.shape[0]
    share = freqs // narrow_count
    piece = share // wide_count
    total_bins = narrow_count * wide_count * GW
    first_freq = narrow_index * share

    near = lax.dynamic_slice_in_dim(spectra, first_freq, share, axis=2)
    gain = lax.dynamic_slice_in_dim(band_gain, first_freq, share, axis=0)

    with jax.named_scope("owner_share_exchange"):
        outgoing = near.reshape(block_rows, 2, wide_count, piece).transpose(2, 0, 1, 3)
        arrived = lax.all_to_all(outgoing, "wide", split_axis=0, concat_axis=0, tiled=True)
        chosen = jnp.stack(
            [lax.dynamic_index_in_dim(arrived, owners[s], 0, keepdims=False) for s in range(steps)]
        )
        copies = jnp.broadcast_to(chosen[None], (wide_count,) + chosen.shape)
        gathered = lax.all_to_all(copies, "wide", split_axis=0, concat_axis=4, tiled=True)

    ids = jnp.stack([pair_near[0], pair_far[0], stack_bins[0]])
    ids = lax.all_gather(ids, "narrow", axis=2, tiled=True)
    near_ids, far_ids = ids[0], ids[1]
    bin_ids = ids[2]

    with jax.named_scope("cross_spectra"):
        parts = []
        for s in range(steps):
            far = gathered[0, s]
            near_rows = select_rows(near, near_ids[s])
            far_rows = select_rows(far, far_ids[s])
            parts.append(lax.optimization_barrier(cross_rows(near_rows, far_rows, gain)))

    with jax.named_scope("bin_sums"):
        real_sum = None
        imag_sum = None
        for s in range(steps):
            bin_hits = (
                jnp.arange(total_bins, dtype=jnp.int32)[:, None] == bin_ids[s][None, :]
            ).astype(jnp.bfloat16)
            real_step = jnp.dot(bin_hits, parts[s][0], preferred_element_type=jnp.float32)
            imag_step = jnp.dot(bin_hits, parts[s][1], preferred_element_type=jnp.float32)
            real_sum = real_step if real_sum is None else real_sum + real_step
            imag_sum = imag_step if imag_sum is None else imag_sum + imag_step

    with jax.named_scope("lag_product"):
        cosine, sine = lag_halves(first_freq, share, freqs, LAGS)
        even = split_product(real_sum, cosine)
        odd = split_product(imag_sum, sine)
        zero_lag = jnp.sum(real_sum, axis=1, keepdims=True)
        last = jnp.arange(LAGS // 2, dtype=jnp.int32)[None, :] == LAGS // 2 - 1
        binned = jnp.stack([even + odd, jnp.where(last, zero_lag, even - odd)])

    with jax.named_scope("bin_exchange"):
        binned = binned.reshape(2, narrow_count, wide_count * GW, LAGS // 2)
        owned = halving_sum(binned, "narrow", narrow_count)
        owned = owned.reshape(2, wide_count, GW, LAGS // 2)
        owned = lax.all_to_all(owned, "wide", split_axis=1, concat_axis=1, tiled=True)
        plus, minus = jnp.sum(owned, axis=1)
        stacked = jnp.concatenate(
            [jnp.flip(plus, axis=1), minus[:, LAGS // 2 - 1 :], minus[:, : LAGS // 2 - 1]], axis=1
        )

    inv_root = 1.0 / freqs**0.5
    stack_scale = (GW / (steps * pair_near.shape[2])) ** 0.5
    return (stacked * (inv_root * stack_scale))[None]


def solution(mesh):
    in_specs = (
        P("wide", None, None),
        P(),
        P(),
        P("wide", None, "narrow"),
        P("wide", None, "narrow"),
        P("wide", None, "narrow"),
    )
    out_specs = P("narrow", "wide", None)
    return jax.shard_map(local, mesh=mesh, in_specs=in_specs, out_specs=out_specs, check_vma=False)
```

```python
import jax
import jax.numpy as jnp
from jax import lax
from jax.sharding import PartitionSpec as P
from jax.experimental import pallas as pl
from jax.experimental.pallas import tpu as pltpu

LAGS = 1024
GW = 8


def trig_pair(freq_values, lag_values, freqs):
    turns = freq_values[:, None] * lag_values[None, :] % (2 * freqs)
    phase = turns.astype(jnp.float32) * (jnp.pi / freqs)
    return (jnp.cos(phase), jnp.sin(phase))


def lag_halves(first_freq, row_count, freqs, lag_count):
    unit_size = 64
    lag_values = jnp.arange(lag_count // 2, dtype=jnp.int32) + 1
    coarse_freq = first_freq + jnp.arange(row_count // unit_size, dtype=jnp.int32) * unit_size
    fine_freq = jnp.arange(unit_size, dtype=jnp.int32)
    coarse_cos, coarse_sin = trig_pair(coarse_freq, lag_values, freqs)
    fine_cos, fine_sin = trig_pair(fine_freq, lag_values, freqs)
    cosine = (
        coarse_cos[:, None, :] * fine_cos[None, :, :]
        - coarse_sin[:, None, :] * fine_sin[None, :, :]
    )
    sine = (
        coarse_sin[:, None, :] * fine_cos[None, :, :]
        + coarse_cos[:, None, :] * fine_sin[None, :, :]
    )
    cosine = cosine.reshape(row_count, lag_count // 2).astype(jnp.bfloat16)
    sine = sine.reshape(row_count, lag_count // 2).astype(jnp.bfloat16)
    return cosine, sine


def select_rows(block, indices):
    block_rows = block.shape[0]
    flat_block = block.reshape(block_rows, -1)
    picker = (indices[:, None] == jnp.arange(block_rows, dtype=jnp.int32)[None, :]).astype(
        jnp.bfloat16
    )
    chosen = jnp.dot(picker, flat_block, preferred_element_type=jnp.bfloat16)
    return chosen.reshape(indices.shape[0], 2, -1)


def cross_rows(near_rows, far_rows, band_gain):
    near_real = near_rows[:, 0].astype(jnp.float32)
    near_imag = near_rows[:, 1].astype(jnp.float32)
    far_real = far_rows[:, 0].astype(jnp.float32)
    far_imag = far_rows[:, 1].astype(jnp.float32)
    real_part = (near_real * far_real + near_imag * far_imag) * band_gain
    imag_part = (near_imag * far_real - near_real * far_imag) * band_gain
    return real_part.astype(jnp.bfloat16), imag_part.astype(jnp.bfloat16)


def split_product(values, table):
    high = lax.reduce_precision(values, exponent_bits=8, mantissa_bits=7)
    low = values - high
    split = jnp.concatenate([high, low], axis=0).astype(jnp.bfloat16)
    both = jnp.dot(split, table, preferred_element_type=jnp.float32)
    return both[: values.shape[0]] + both[values.shape[0] :]


def halving_sum(parts, axis, count):
    index = lax.axis_index(axis)
    bit = 1
    while bit < count:
        mine = (index // bit) % 2
        paired = parts.reshape((parts.shape[0], parts.shape[1] // 2, 2) + parts.shape[2:])
        first, second = paired[:, :, 0], paired[:, :, 1]
        keep = jnp.where(mine == 0, first, second)
        send = jnp.where(mine == 0, second, first)
        pairs = [(i, i ^ bit) for i in range(count)]
        parts = keep + lax.ppermute(send, axis, pairs)
        bit *= 2
    return parts[:, 0]


def bin_cross_kernel(near_re, near_im, far_re, far_im, far_pick, gain, bin_pick, out_re, out_im):
    step = pl.program_id(1)
    picker = far_pick[0]
    far_real = jnp.dot(picker, far_re[0], preferred_element_type=jnp.float32)
    far_imag = jnp.dot(picker, far_im[0], preferred_element_type=jnp.float32)
    near_real = near_re[0].astype(jnp.float32)
    near_imag = near_im[0].astype(jnp.float32)
    weight = gain[...]
    real_part = ((near_real * far_real + near_imag * far_imag) * weight).astype(jnp.bfloat16)
    imag_part = ((near_imag * far_real - near_real * far_imag) * weight).astype(jnp.bfloat16)
    bins = bin_pick[0]
    real_sum = jnp.dot(bins, real_part, preferred_element_type=jnp.float32)
    imag_sum = jnp.dot(bins, imag_part, preferred_element_type=jnp.float32)

    @pl.when(step == 0)
    def _():
        out_re[...] = real_sum
        out_im[...] = imag_sum

    @pl.when(step > 0)
    def _():
        out_re[...] += real_sum
        out_im[...] += imag_sum


def bin_cross(near_rows, far_blocks, far_pick, gain, bin_pick, tile):
    steps, pairs, width = near_rows.shape
    share = width // 2
    block_rows = far_blocks.shape[1]
    bins = bin_pick.shape[1]
    tiles = share // tile
    row_spec = lambda offset: pl.BlockSpec((1, pairs, tile), lambda t, s: (s, 0, t + offset))
    block_spec = lambda offset: pl.BlockSpec((1, block_rows, tile), lambda t, s: (s, 0, t + offset))
    out_spec = pl.BlockSpec((bins, tile), lambda t, s: (0, t))
    return pl.pallas_call(
        bin_cross_kernel,
        grid=(tiles, steps),
        in_specs=[
            row_spec(0),
            row_spec(tiles),
            block_spec(0),
            block_spec(tiles),
            pl.BlockSpec((1, pairs, block_rows), lambda t, s: (s, 0, 0)),
            pl.BlockSpec((1, tile), lambda t, s: (0, t)),
            pl.BlockSpec((1, bins, pairs), lambda t, s: (s, 0, 0)),
        ],
        out_specs=[out_spec, out_spec],
        out_shape=[jax.ShapeDtypeStruct((bins, share), jnp.float32)] * 2,
        compiler_params=pltpu.CompilerParams(dimension_semantics=("parallel", "arbitrary")),
        cost_estimate=pl.CostEstimate(
            flops=2 * steps * share * (2 * pairs * block_rows + 2 * bins * pairs),
            transcendentals=0,
            bytes_accessed=2 * steps * pairs * width + 2 * steps * block_rows * width + 8 * bins * share,
        ),
    )(near_rows, near_rows, far_blocks, far_blocks, far_pick, gain, bin_pick)


def local(spectra, band_gain, owners, pair_near, pair_far, stack_bins):
    narrow_count = lax.axis_size("narrow")
    wide_count = lax.axis_size("wide")
    narrow_index = lax.axis_index("narrow")
    block_rows, _, freqs = spectra.shape
    steps = owners.shape[0]
    share = freqs // narrow_count
    piece = share // wide_count
    total_bins = narrow_count * wide_count * GW
    first_freq = narrow_index * share

    near = lax.dynamic_slice_in_dim(spectra, first_freq, share, axis=2)
    gain = lax.dynamic_slice_in_dim(band_gain, first_freq, share, axis=0)

    with jax.named_scope("owner_share_exchange"):
        outgoing = near.reshape(block_rows, 2, wide_count, piece).transpose(2, 0, 1, 3)
        arrived = lax.all_to_all(outgoing, "wide", split_axis=0, concat_axis=0, tiled=True)
        chosen = jnp.stack(
            [lax.dynamic_index_in_dim(arrived, owners[s], 0, keepdims=False) for s in range(steps)]
        )
        copies = jnp.broadcast_to(chosen[None], (wide_count,) + chosen.shape)
        gathered = lax.all_to_all(copies, "wide", split_axis=0, concat_axis=4, tiled=True)

    ids = jnp.stack([pair_near[0], pair_far[0], stack_bins[0]])
    ids = lax.all_gather(ids, "narrow", axis=2, tiled=True)
    near_ids, far_ids = ids[0], ids[1]
    bin_ids = ids[2]

    with jax.named_scope("near_rows"):
        near_rows = jnp.stack(
            [select_rows(near, near_ids[s]).reshape(near_ids.shape[1], 2 * share) for s in range(steps)]
        )
        rows = jnp.arange(block_rows, dtype=jnp.int32)[None, None, :]
        far_pick = (far_ids[:, :, None] == rows).astype(jnp.bfloat16)
        bins = jnp.arange(total_bins, dtype=jnp.int32)[None, :, None]
        bin_pick = (bins == bin_ids[:, None, :]).astype(jnp.bfloat16)

    with jax.named_scope("bin_cross"):
        far_blocks = gathered[0].reshape(steps, block_rows, 2 * share)
        real_sum, imag_sum = bin_cross(
            near_rows, far_blocks, far_pick, gain.reshape(1, share), bin_pick, 512
        )

    with jax.named_scope("lag_product"):
        cosine, sine = lag_halves(first_freq, share, freqs, LAGS)
        even = split_product(real_sum, cosine)
        odd = split_product(imag_sum, sine)
        zero_lag = jnp.sum(real_sum, axis=1, keepdims=True)
        last = jnp.arange(LAGS // 2, dtype=jnp.int32)[None, :] == LAGS // 2 - 1
        binned = jnp.stack([even + odd, jnp.where(last, zero_lag, even - odd)])

    with jax.named_scope("bin_exchange"):
        binned = binned.reshape(2, narrow_count, wide_count * GW, LAGS // 2)
        owned = halving_sum(binned, "narrow", narrow_count)
        owned = owned.reshape(2, wide_count, GW, LAGS // 2)
        owned = lax.all_to_all(owned, "wide", split_axis=1, concat_axis=1, tiled=True)
        plus, minus = jnp.sum(owned, axis=1)
        stacked = jnp.concatenate(
            [jnp.flip(plus, axis=1), minus[:, LAGS // 2 - 1 :], minus[:, : LAGS // 2 - 1]], axis=1
        )

    inv_root = 1.0 / freqs**0.5
    stack_scale = (GW / (steps * pair_near.shape[2])) ** 0.5
    return (stacked * (inv_root * stack_scale))[None]


def solution(mesh):
    in_specs = (
        P("wide", None, None),
        P(),
        P(),
        P("wide", None, "narrow"),
        P("wide", None, "narrow"),
        P("wide", None, "narrow"),
    )
    out_specs = P("narrow", "wide", None)
    return jax.shard_map(local, mesh=mesh, in_specs=in_specs, out_specs=out_specs, check_vma=False)
```

```python
import jax
import jax.numpy as jnp
from jax import lax
from jax.sharding import PartitionSpec as P

LAGS = 1024
GW = 8


def trig_pair(freq_values, lag_values, freqs):
    turns = freq_values[:, None] * lag_values[None, :] % (2 * freqs)
    phase = turns.astype(jnp.float32) * (jnp.pi / freqs)
    return (jnp.cos(phase), jnp.sin(phase))


def lag_halves(first_freq, row_count, freqs, lag_count):
    unit_size = 64
    lag_values = jnp.arange(lag_count // 2, dtype=jnp.int32) + 1
    coarse_freq = first_freq + jnp.arange(row_count // unit_size, dtype=jnp.int32) * unit_size
    fine_freq = jnp.arange(unit_size, dtype=jnp.int32)
    coarse_cos, coarse_sin = trig_pair(coarse_freq, lag_values, freqs)
    fine_cos, fine_sin = trig_pair(fine_freq, lag_values, freqs)
    cosine = (
        coarse_cos[:, None, :] * fine_cos[None, :, :]
        - coarse_sin[:, None, :] * fine_sin[None, :, :]
    )
    sine = (
        coarse_sin[:, None, :] * fine_cos[None, :, :]
        + coarse_cos[:, None, :] * fine_sin[None, :, :]
    )
    cosine = cosine.reshape(row_count, lag_count // 2).astype(jnp.bfloat16)
    sine = sine.reshape(row_count, lag_count // 2).astype(jnp.bfloat16)
    return cosine, sine


def select_rows(block, indices):
    block_rows = block.shape[0]
    flat_block = block.reshape(block_rows, -1)
    picker = (indices[:, None] == jnp.arange(block_rows, dtype=jnp.int32)[None, :]).astype(
        jnp.bfloat16
    )
    chosen = jnp.dot(picker, flat_block, preferred_element_type=jnp.bfloat16)
    return chosen.reshape(indices.shape[0], 2, -1)


def cross_rows(near_rows, far_rows, band_gain):
    near_real = near_rows[:, 0].astype(jnp.float32)
    near_imag = near_rows[:, 1].astype(jnp.float32)
    far_real = far_rows[:, 0].astype(jnp.float32)
    far_imag = far_rows[:, 1].astype(jnp.float32)
    real_part = (near_real * far_real + near_imag * far_imag) * band_gain
    imag_part = (near_imag * far_real - near_real * far_imag) * band_gain
    return real_part.astype(jnp.bfloat16), imag_part.astype(jnp.bfloat16)


def split_product(values, table):
    high = lax.reduce_precision(values, exponent_bits=8, mantissa_bits=7)
    low = values - high
    split = jnp.concatenate([high, low], axis=0).astype(jnp.bfloat16)
    both = jnp.dot(split, table, preferred_element_type=jnp.float32)
    return both[: values.shape[0]] + both[values.shape[0] :]


def halving_sum(parts, axis, count):
    index = lax.axis_index(axis)
    bit = 1
    while bit < count:
        mine = (index // bit) % 2
        paired = parts.reshape((parts.shape[0], parts.shape[1] // 2, 2) + parts.shape[2:])
        first, second = paired[:, :, 0], paired[:, :, 1]
        keep = jnp.where(mine == 0, first, second)
        send = jnp.where(mine == 0, second, first)
        pairs = [(i, i ^ bit) for i in range(count)]
        parts = keep + lax.ppermute(send, axis, pairs)
        bit *= 2
    return parts[:, 0]


def local(spectra, band_gain, owners, pair_near, pair_far, stack_bins):
    narrow_count = lax.axis_size("narrow")
    wide_count = lax.axis_size("wide")
    narrow_index = lax.axis_index("narrow")
    block_rows, _, freqs = spectra.shape
    steps = owners.shape[0]
    share = freqs // narrow_count
    piece = share // wide_count
    total_bins = narrow_count * wide_count * GW
    first_freq = narrow_index * share

    near = lax.dynamic_slice_in_dim(spectra, first_freq, share, axis=2)
    gain = lax.dynamic_slice_in_dim(band_gain, first_freq, share, axis=0)

    with jax.named_scope("owner_share_exchange"):
        outgoing = near.reshape(block_rows, 2, wide_count, piece).transpose(2, 0, 1, 3)
        arrived = lax.all_to_all(outgoing, "wide", split_axis=0, concat_axis=0, tiled=True)
        chosen = [
            lax.dynamic_index_in_dim(arrived, owners[s], 0, keepdims=False) for s in range(steps)
        ]

    ids = jnp.stack([pair_near[0], pair_far[0], stack_bins[0]])
    ids = lax.all_gather(ids, "narrow", axis=2, tiled=True)
    near_ids, far_ids = ids[0], ids[1]
    bin_ids = ids[2]

    with jax.named_scope("near_rows"):
        near_rows = [select_rows(near, near_ids[s]) for s in range(steps)]

    sums = None
    for s in range(steps):
        with jax.named_scope("owner_share_gather"):
            copies = jnp.broadcast_to(chosen[s][None], (wide_count,) + chosen[s].shape)
            gathered = lax.all_to_all(copies, "wide", split_axis=0, concat_axis=3, tiled=True)
            if sums is not None:
                gathered, sums = lax.optimization_barrier((gathered, sums))
        with jax.named_scope("cross_spectra"):
            far_rows = select_rows(gathered[0], far_ids[s])
            real_part, imag_part = lax.optimization_barrier(cross_rows(near_rows[s], far_rows, gain))
        with jax.named_scope("bin_sums"):
            bin_hits = (
                jnp.arange(total_bins, dtype=jnp.int32)[:, None] == bin_ids[s][None, :]
            ).astype(jnp.bfloat16)
            real_step = jnp.dot(bin_hits, real_part, preferred_element_type=jnp.float32)
            imag_step = jnp.dot(bin_hits, imag_part, preferred_element_type=jnp.float32)
            if sums is None:
                sums = (real_step, imag_step)
            else:
                sums = (sums[0] + real_step, sums[1] + imag_step)
    real_sum, imag_sum = sums

    with jax.named_scope("lag_product"):
        cosine, sine = lag_halves(first_freq, share, freqs, LAGS)
        even = split_product(real_sum, cosine)
        odd = split_product(imag_sum, sine)
        zero_lag = jnp.sum(real_sum, axis=1, keepdims=True)
        last = jnp.arange(LAGS // 2, dtype=jnp.int32)[None, :] == LAGS // 2 - 1
        binned = jnp.stack([even + odd, jnp.where(last, zero_lag, even - odd)])

    with jax.named_scope("bin_exchange"):
        binned = binned.reshape(2, narrow_count, wide_count * GW, LAGS // 2)
        owned = halving_sum(binned, "narrow", narrow_count)
        owned = owned.reshape(2, wide_count, GW, LAGS // 2)
        owned = lax.all_to_all(owned, "wide", split_axis=1, concat_axis=1, tiled=True)
        plus, minus = jnp.sum(owned, axis=1)
        stacked = jnp.concatenate(
            [jnp.flip(plus, axis=1), minus[:, LAGS // 2 - 1 :], minus[:, : LAGS // 2 - 1]], axis=1
        )

    inv_root = 1.0 / freqs**0.5
    stack_scale = (GW / (steps * pair_near.shape[2])) ** 0.5
    return (stacked * (inv_root * stack_scale))[None]


def solution(mesh):
    in_specs = (
        P("wide", None, None),
        P(),
        P(),
        P("wide", None, "narrow"),
        P("wide", None, "narrow"),
        P("wide", None, "narrow"),
    )
    out_specs = P("narrow", "wide", None)
    return jax.shard_map(local, mesh=mesh, in_specs=in_specs, out_specs=out_specs, check_vma=False)
```

```python
import jax
import jax.numpy as jnp
from jax import lax
from jax.sharding import PartitionSpec as P

LAGS = 1024
GW = 8


def trig_pair(freq_values, lag_values, freqs):
    turns = freq_values[:, None] * lag_values[None, :] % (2 * freqs)
    phase = turns.astype(jnp.float32) * (jnp.pi / freqs)
    return (jnp.cos(phase), jnp.sin(phase))


def lag_halves(first_freq, row_count, freqs, lag_count):
    unit_size = 64
    lag_values = jnp.arange(lag_count // 2, dtype=jnp.int32) + 1
    coarse_freq = first_freq + jnp.arange(row_count // unit_size, dtype=jnp.int32) * unit_size
    fine_freq = jnp.arange(unit_size, dtype=jnp.int32)
    coarse_cos, coarse_sin = trig_pair(coarse_freq, lag_values, freqs)
    fine_cos, fine_sin = trig_pair(fine_freq, lag_values, freqs)
    cosine = (
        coarse_cos[:, None, :] * fine_cos[None, :, :]
        - coarse_sin[:, None, :] * fine_sin[None, :, :]
    )
    sine = (
        coarse_sin[:, None, :] * fine_cos[None, :, :]
        + coarse_cos[:, None, :] * fine_sin[None, :, :]
    )
    cosine = cosine.reshape(row_count, lag_count // 2).astype(jnp.bfloat16)
    sine = sine.reshape(row_count, lag_count // 2).astype(jnp.bfloat16)
    return cosine, sine


def select_rows(block, indices):
    block_rows = block.shape[0]
    flat_block = block.reshape(block_rows, -1)
    picker = (indices[:, None] == jnp.arange(block_rows, dtype=jnp.int32)[None, :]).astype(
        jnp.bfloat16
    )
    chosen = jnp.dot(picker, flat_block, preferred_element_type=jnp.bfloat16)
    return chosen.reshape(indices.shape[0], 2, -1)


def pick_rows(block, indices):
    picker = (indices[:, None] == jnp.arange(block.shape[0], dtype=jnp.int32)[None, :]).astype(
        jnp.bfloat16
    )
    return jnp.dot(picker, block, preferred_element_type=jnp.bfloat16)


def cross_rows(near_rows, far_real, far_imag, band_gain):
    near_real = near_rows[:, 0].astype(jnp.float32)
    near_imag = near_rows[:, 1].astype(jnp.float32)
    far_real = far_real.astype(jnp.float32)
    far_imag = far_imag.astype(jnp.float32)
    real_part = (near_real * far_real + near_imag * far_imag) * band_gain
    imag_part = (near_imag * far_real - near_real * far_imag) * band_gain
    return real_part.astype(jnp.bfloat16), imag_part.astype(jnp.bfloat16)


def split_product(values, table):
    high = lax.reduce_precision(values, exponent_bits=8, mantissa_bits=7)
    low = values - high
    split = jnp.concatenate([high, low], axis=0).astype(jnp.bfloat16)
    both = jnp.dot(split, table, preferred_element_type=jnp.float32)
    return both[: values.shape[0]] + both[values.shape[0] :]


def halving_sum(parts, axis, count):
    index = lax.axis_index(axis)
    bit = 1
    while bit < count:
        mine = (index // bit) % 2
        paired = parts.reshape((parts.shape[0], parts.shape[1] // 2, 2) + parts.shape[2:])
        first, second = paired[:, :, 0], paired[:, :, 1]
        keep = jnp.where(mine == 0, first, second)
        send = jnp.where(mine == 0, second, first)
        pairs = [(i, i ^ bit) for i in range(count)]
        parts = keep + lax.ppermute(send, axis, pairs)
        bit *= 2
    return parts[:, 0]


def local(spectra, band_gain, owners, pair_near, pair_far, stack_bins):
    narrow_count = lax.axis_size("narrow")
    wide_count = lax.axis_size("wide")
    narrow_index = lax.axis_index("narrow")
    block_rows, _, freqs = spectra.shape
    steps = owners.shape[0]
    share = freqs // narrow_count
    piece = share // wide_count
    total_bins = narrow_count * wide_count * GW
    first_freq = narrow_index * share

    near = lax.dynamic_slice_in_dim(spectra, first_freq, share, axis=2)
    gain = lax.dynamic_slice_in_dim(band_gain, first_freq, share, axis=0)

    with jax.named_scope("owner_share_exchange"):
        outgoing = near.reshape(block_rows, 2, wide_count, piece).transpose(2, 1, 0, 3)
        arrived = lax.all_to_all(outgoing, "wide", split_axis=0, concat_axis=0, tiled=True)
        chosen = jnp.stack(
            [lax.dynamic_index_in_dim(arrived, owners[s], 0, keepdims=False) for s in range(steps)]
        )
        copies = jnp.broadcast_to(chosen[None], (wide_count,) + chosen.shape)
        gathered = lax.all_to_all(copies, "wide", split_axis=0, concat_axis=4, tiled=True)

    ids = jnp.stack([pair_near[0], pair_far[0], stack_bins[0]])
    ids = lax.all_gather(ids, "narrow", axis=2, tiled=True)
    near_ids, far_ids = ids[0], ids[1]
    bin_ids = ids[2]

    with jax.named_scope("cross_spectra"):
        parts = []
        for s in range(steps):
            near_rows = select_rows(near, near_ids[s])
            far_real = pick_rows(gathered[0, s, 0], far_ids[s])
            far_imag = pick_rows(gathered[0, s, 1], far_ids[s])
            parts.append(
                lax.optimization_barrier(cross_rows(near_rows, far_real, far_imag, gain))
            )

    with jax.named_scope("bin_sums"):
        real_sum = None
        imag_sum = None
        for s in range(steps):
            bin_hits = (
                jnp.arange(total_bins, dtype=jnp.int32)[:, None] == bin_ids[s][None, :]
            ).astype(jnp.bfloat16)
            real_step = jnp.dot(bin_hits, parts[s][0], preferred_element_type=jnp.float32)
            imag_step = jnp.dot(bin_hits, parts[s][1], preferred_element_type=jnp.float32)
            real_sum = real_step if real_sum is None else real_sum + real_step
            imag_sum = imag_step if imag_sum is None else imag_sum + imag_step

    with jax.named_scope("lag_product"):
        cosine, sine = lag_halves(first_freq, share, freqs, LAGS)
        even = split_product(real_sum, cosine)
        odd = split_product(imag_sum, sine)
        zero_lag = jnp.sum(real_sum, axis=1, keepdims=True)
        last = jnp.arange(LAGS // 2, dtype=jnp.int32)[None, :] == LAGS // 2 - 1
        binned = jnp.stack([even + odd, jnp.where(last, zero_lag, even - odd)])

    with jax.named_scope("bin_exchange"):
        binned = binned.reshape(2, narrow_count, wide_count * GW, LAGS // 2)
        owned = halving_sum(binned, "narrow", narrow_count)
        owned = owned.reshape(2, wide_count, GW, LAGS // 2)
        owned = lax.all_to_all(owned, "wide", split_axis=1, concat_axis=1, tiled=True)
        plus, minus = jnp.sum(owned, axis=1)
        stacked = jnp.concatenate(
            [jnp.flip(plus, axis=1), minus[:, LAGS // 2 - 1 :], minus[:, : LAGS // 2 - 1]], axis=1
        )

    inv_root = 1.0 / freqs**0.5
    stack_scale = (GW / (steps * pair_near.shape[2])) ** 0.5
    return (stacked * (inv_root * stack_scale))[None]


def solution(mesh):
    in_specs = (
        P("wide", None, None),
        P(),
        P(),
        P("wide", None, "narrow"),
        P("wide", None, "narrow"),
        P("wide", None, "narrow"),
    )
    out_specs = P("narrow", "wide", None)
    return jax.shard_map(local, mesh=mesh, in_specs=in_specs, out_specs=out_specs, check_vma=False)
```

```python
import jax
import jax.numpy as jnp
from jax import lax
from jax.sharding import PartitionSpec as P

LAGS = 1024
GW = 8


def trig_pair(freq_values, lag_values, freqs):
    turns = freq_values[:, None] * lag_values[None, :] % (2 * freqs)
    phase = turns.astype(jnp.float32) * (jnp.pi / freqs)
    return (jnp.cos(phase), jnp.sin(phase))


def lag_halves(first_freq, row_count, freqs, lag_count):
    unit_size = 64
    lag_values = jnp.arange(lag_count // 2, dtype=jnp.int32) + 1
    coarse_freq = first_freq + jnp.arange(row_count // unit_size, dtype=jnp.int32) * unit_size
    fine_freq = jnp.arange(unit_size, dtype=jnp.int32)
    coarse_cos, coarse_sin = trig_pair(coarse_freq, lag_values, freqs)
    fine_cos, fine_sin = trig_pair(fine_freq, lag_values, freqs)
    cosine = (
        coarse_cos[:, None, :] * fine_cos[None, :, :]
        - coarse_sin[:, None, :] * fine_sin[None, :, :]
    )
    sine = (
        coarse_sin[:, None, :] * fine_cos[None, :, :]
        + coarse_cos[:, None, :] * fine_sin[None, :, :]
    )
    cosine = cosine.reshape(row_count, lag_count // 2).astype(jnp.bfloat16)
    sine = sine.reshape(row_count, lag_count // 2).astype(jnp.bfloat16)
    return cosine, sine


def select_rows(block, indices):
    block_rows = block.shape[0]
    flat_block = block.reshape(block_rows, -1)
    picker = (indices[:, None] == jnp.arange(block_rows, dtype=jnp.int32)[None, :]).astype(
        jnp.bfloat16
    )
    chosen = jnp.dot(picker, flat_block, preferred_element_type=jnp.bfloat16)
    return chosen.reshape(indices.shape[0], 2, -1)


def pick_rows(block, indices):
    picker = (indices[:, None] == jnp.arange(block.shape[0], dtype=jnp.int32)[None, :]).astype(
        jnp.bfloat16
    )
    return jnp.dot(picker, block, preferred_element_type=jnp.bfloat16)


def cross_rows(near_rows, far_real, far_imag, band_gain):
    near_real = near_rows[:, 0].astype(jnp.float32)
    near_imag = near_rows[:, 1].astype(jnp.float32)
    far_real = far_real.astype(jnp.float32)
    far_imag = far_imag.astype(jnp.float32)
    real_part = (near_real * far_real + near_imag * far_imag) * band_gain
    imag_part = (near_imag * far_real - near_real * far_imag) * band_gain
    return real_part.astype(jnp.bfloat16), imag_part.astype(jnp.bfloat16)


def split_product(values, table):
    high = lax.reduce_precision(values, exponent_bits=8, mantissa_bits=7)
    low = values - high
    split = jnp.concatenate([high, low], axis=0).astype(jnp.bfloat16)
    both = jnp.dot(split, table, preferred_element_type=jnp.float32)
    return both[: values.shape[0]] + both[values.shape[0] :]


def halving_sum(parts, axis, count):
    index = lax.axis_index(axis)
    bit = 1
    while bit < count:
        mine = (index // bit) % 2
        paired = parts.reshape((parts.shape[0], parts.shape[1] // 2, 2) + parts.shape[2:])
        first, second = paired[:, :, 0], paired[:, :, 1]
        keep = jnp.where(mine == 0, first, second)
        send = jnp.where(mine == 0, second, first)
        pairs = [(i, i ^ bit) for i in range(count)]
        parts = keep + lax.ppermute(send, axis, pairs)
        bit *= 2
    return parts[:, 0]


def local(spectra, band_gain, owners, pair_near, pair_far, stack_bins):
    narrow_count = lax.axis_size("narrow")
    wide_count = lax.axis_size("wide")
    narrow_index = lax.axis_index("narrow")
    block_rows, _, freqs = spectra.shape
    steps = owners.shape[0]
    share = freqs // narrow_count
    piece = share // wide_count
    total_bins = narrow_count * wide_count * GW
    first_freq = narrow_index * share

    near = lax.dynamic_slice_in_dim(spectra, first_freq, share, axis=2)
    gain = lax.dynamic_slice_in_dim(band_gain, first_freq, share, axis=0)

    with jax.named_scope("owner_share_exchange"):
        outgoing = lax.dynamic_index_in_dim(
            spectra.reshape(block_rows, 2, narrow_count, wide_count, piece),
            narrow_index,
            2,
            keepdims=False,
        ).transpose(2, 1, 0, 3)
        arrived = lax.all_to_all(outgoing, "wide", split_axis=0, concat_axis=0, tiled=True)
        chosen = jnp.stack(
            [lax.dynamic_index_in_dim(arrived, owners[s], 0, keepdims=False) for s in range(steps)]
        )
        copies = jnp.broadcast_to(chosen[None], (wide_count,) + chosen.shape)
        gathered = lax.all_to_all(copies, "wide", split_axis=0, concat_axis=4, tiled=True)

    ids = jnp.stack([pair_near[0], pair_far[0], stack_bins[0]])
    ids = lax.all_gather(ids, "narrow", axis=2, tiled=True)
    near_ids, far_ids = ids[0], ids[1]
    bin_ids = ids[2]

    with jax.named_scope("cross_spectra"):
        parts = []
        for s in range(steps):
            near_rows = select_rows(near, near_ids[s])
            far_real = pick_rows(gathered[0, s, 0], far_ids[s])
            far_imag = pick_rows(gathered[0, s, 1], far_ids[s])
            parts.append(
                lax.optimization_barrier(cross_rows(near_rows, far_real, far_imag, gain))
            )

    with jax.named_scope("bin_sums"):
        real_sum = None
        imag_sum = None
        for s in range(steps):
            bin_hits = (
                jnp.arange(total_bins, dtype=jnp.int32)[:, None] == bin_ids[s][None, :]
            ).astype(jnp.bfloat16)
            real_step = jnp.dot(bin_hits, parts[s][0], preferred_element_type=jnp.float32)
            imag_step = jnp.dot(bin_hits, parts[s][1], preferred_element_type=jnp.float32)
            real_sum = real_step if real_sum is None else real_sum + real_step
            imag_sum = imag_step if imag_sum is None else imag_sum + imag_step

    with jax.named_scope("lag_product"):
        cosine, sine = lag_halves(first_freq, share, freqs, LAGS)
        even = split_product(real_sum, cosine)
        odd = split_product(imag_sum, sine)
        zero_lag = jnp.sum(real_sum, axis=1, keepdims=True)
        last = jnp.arange(LAGS // 2, dtype=jnp.int32)[None, :] == LAGS // 2 - 1
        binned = jnp.stack([even + odd, jnp.where(last, zero_lag, even - odd)])

    with jax.named_scope("bin_exchange"):
        binned = binned.reshape(2, narrow_count, wide_count * GW, LAGS // 2)
        owned = halving_sum(binned, "narrow", narrow_count)
        owned = owned.reshape(2, wide_count, GW, LAGS // 2)
        owned = lax.all_to_all(owned, "wide", split_axis=1, concat_axis=1, tiled=True)
        plus, minus = jnp.sum(owned, axis=1)
        stacked = jnp.concatenate(
            [jnp.flip(plus, axis=1), minus[:, LAGS // 2 - 1 :], minus[:, : LAGS // 2 - 1]], axis=1
        )

    inv_root = 1.0 / freqs**0.5
    stack_scale = (GW / (steps * pair_near.shape[2])) ** 0.5
    return (stacked * (inv_root * stack_scale))[None]


def solution(mesh):
    in_specs = (
        P("wide", None, None),
        P(),
        P(),
        P("wide", None, "narrow"),
        P("wide", None, "narrow"),
        P("wide", None, "narrow"),
    )
    out_specs = P("narrow", "wide", None)
    return jax.shard_map(local, mesh=mesh, in_specs=in_specs, out_specs=out_specs, check_vma=False)
```

```python
import jax
import jax.numpy as jnp
from jax import lax
from jax.sharding import PartitionSpec as P

LAGS = 1024
GW = 8


def trig_pair(freq_values, lag_values, freqs):
    turns = freq_values[:, None] * lag_values[None, :] % (2 * freqs)
    phase = turns.astype(jnp.float32) * (jnp.pi / freqs)
    return (jnp.cos(phase), jnp.sin(phase))


def lag_halves(first_freq, row_count, freqs, lag_count):
    unit_size = 64
    lag_values = jnp.arange(lag_count // 2, dtype=jnp.int32) + 1
    coarse_freq = first_freq + jnp.arange(row_count // unit_size, dtype=jnp.int32) * unit_size
    fine_freq = jnp.arange(unit_size, dtype=jnp.int32)
    coarse_cos, coarse_sin = trig_pair(coarse_freq, lag_values, freqs)
    fine_cos, fine_sin = trig_pair(fine_freq, lag_values, freqs)
    cosine = (
        coarse_cos[:, None, :] * fine_cos[None, :, :]
        - coarse_sin[:, None, :] * fine_sin[None, :, :]
    )
    sine = (
        coarse_sin[:, None, :] * fine_cos[None, :, :]
        + coarse_cos[:, None, :] * fine_sin[None, :, :]
    )
    cosine = cosine.reshape(row_count, lag_count // 2).astype(jnp.bfloat16)
    sine = sine.reshape(row_count, lag_count // 2).astype(jnp.bfloat16)
    return cosine, sine


def select_rows(block, indices):
    block_rows = block.shape[0]
    flat_block = block.reshape(block_rows, -1)
    picker = (indices[:, None] == jnp.arange(block_rows, dtype=jnp.int32)[None, :]).astype(
        jnp.bfloat16
    )
    chosen = jnp.dot(picker, flat_block, preferred_element_type=jnp.bfloat16)
    return chosen.reshape(indices.shape[0], 2, -1)


def pick_rows(block, indices):
    picker = (indices[:, None] == jnp.arange(block.shape[0], dtype=jnp.int32)[None, :]).astype(
        jnp.bfloat16
    )
    return jnp.dot(picker, block, preferred_element_type=jnp.bfloat16)


def cross_rows(near_rows, far_real, far_imag, band_gain):
    near_real = near_rows[:, 0].astype(jnp.float32)
    near_imag = near_rows[:, 1].astype(jnp.float32)
    far_real = far_real.astype(jnp.float32)
    far_imag = far_imag.astype(jnp.float32)
    real_part = (near_real * far_real + near_imag * far_imag) * band_gain
    imag_part = (near_imag * far_real - near_real * far_imag) * band_gain
    return real_part.astype(jnp.bfloat16), imag_part.astype(jnp.bfloat16)


def split_product(values, table):
    high = lax.reduce_precision(values, exponent_bits=8, mantissa_bits=7)
    low = values - high
    split = jnp.concatenate([high, low], axis=0).astype(jnp.bfloat16)
    both = jnp.dot(split, table, preferred_element_type=jnp.float32)
    return both[: values.shape[0]] + both[values.shape[0] :]


def halving_sum(parts, axis, count):
    index = lax.axis_index(axis)
    bit = 1
    while bit < count:
        mine = (index // bit) % 2
        paired = parts.reshape((parts.shape[0], parts.shape[1] // 2, 2) + parts.shape[2:])
        first, second = paired[:, :, 0], paired[:, :, 1]
        keep = jnp.where(mine == 0, first, second)
        send = jnp.where(mine == 0, second, first)
        pairs = [(i, i ^ bit) for i in range(count)]
        parts = keep + lax.ppermute(send, axis, pairs)
        bit *= 2
    return parts[:, 0]


def local(spectra, band_gain, owners, pair_near, pair_far, stack_bins):
    narrow_count = lax.axis_size("narrow")
    wide_count = lax.axis_size("wide")
    narrow_index = lax.axis_index("narrow")
    block_rows, _, freqs = spectra.shape
    steps = owners.shape[0]
    share = freqs // narrow_count
    total_bins = narrow_count * wide_count * GW
    first_freq = narrow_index * share

    near = lax.dynamic_slice_in_dim(spectra, first_freq, share, axis=2)
    gain = lax.dynamic_slice_in_dim(band_gain, first_freq, share, axis=0)

    with jax.named_scope("owner_share_exchange"):
        group = block_rows // wide_count
        outgoing = near.reshape(wide_count, group, 2, share)
        arrived = lax.all_to_all(outgoing, "wide", split_axis=0, concat_axis=0, tiled=True)
        chosen = jnp.stack(
            [lax.dynamic_index_in_dim(arrived, owners[s], 0, keepdims=False) for s in range(steps)]
        )
        copies = jnp.broadcast_to(chosen[None], (wide_count,) + chosen.shape)
        gathered = lax.all_to_all(copies, "wide", split_axis=0, concat_axis=0, tiled=True)
        far_blocks = [
            gathered[:, s].reshape(block_rows, 2, share) for s in range(steps)
        ]

    ids = jnp.stack([pair_near[0], pair_far[0], stack_bins[0]])
    ids = lax.all_gather(ids, "narrow", axis=2, tiled=True)
    near_ids, far_ids = ids[0], ids[1]
    bin_ids = ids[2]

    with jax.named_scope("cross_spectra"):
        parts = []
        for s in range(steps):
            near_rows = select_rows(near, near_ids[s])
            far_real = pick_rows(far_blocks[s][:, 0], far_ids[s])
            far_imag = pick_rows(far_blocks[s][:, 1], far_ids[s])
            parts.append(
                lax.optimization_barrier(cross_rows(near_rows, far_real, far_imag, gain))
            )

    with jax.named_scope("bin_sums"):
        real_sum = None
        imag_sum = None
        for s in range(steps):
            bin_hits = (
                jnp.arange(total_bins, dtype=jnp.int32)[:, None] == bin_ids[s][None, :]
            ).astype(jnp.bfloat16)
            real_step = jnp.dot(bin_hits, parts[s][0], preferred_element_type=jnp.float32)
            imag_step = jnp.dot(bin_hits, parts[s][1], preferred_element_type=jnp.float32)
            real_sum = real_step if real_sum is None else real_sum + real_step
            imag_sum = imag_step if imag_sum is None else imag_sum + imag_step

    with jax.named_scope("lag_product"):
        cosine, sine = lag_halves(first_freq, share, freqs, LAGS)
        even = split_product(real_sum, cosine)
        odd = split_product(imag_sum, sine)
        zero_lag = jnp.sum(real_sum, axis=1, keepdims=True)
        last = jnp.arange(LAGS // 2, dtype=jnp.int32)[None, :] == LAGS // 2 - 1
        binned = jnp.stack([even + odd, jnp.where(last, zero_lag, even - odd)])

    with jax.named_scope("bin_exchange"):
        binned = binned.reshape(2, narrow_count, wide_count * GW, LAGS // 2)
        owned = halving_sum(binned, "narrow", narrow_count)
        owned = owned.reshape(2, wide_count, GW, LAGS // 2)
        owned = lax.all_to_all(owned, "wide", split_axis=1, concat_axis=1, tiled=True)
        plus, minus = jnp.sum(owned, axis=1)
        stacked = jnp.concatenate(
            [jnp.flip(plus, axis=1), minus[:, LAGS // 2 - 1 :], minus[:, : LAGS // 2 - 1]], axis=1
        )

    inv_root = 1.0 / freqs**0.5
    stack_scale = (GW / (steps * pair_near.shape[2])) ** 0.5
    return (stacked * (inv_root * stack_scale))[None]


def solution(mesh):
    in_specs = (
        P("wide", None, None),
        P(),
        P(),
        P("wide", None, "narrow"),
        P("wide", None, "narrow"),
        P("wide", None, "narrow"),
    )
    out_specs = P("narrow", "wide", None)
    return jax.shard_map(local, mesh=mesh, in_specs=in_specs, out_specs=out_specs, check_vma=False)
```

```python
import jax
import jax.numpy as jnp
from jax import lax
from jax.sharding import PartitionSpec as P

LAGS = 1024
GW = 8


def trig_pair(freq_values, lag_values, freqs):
    turns = freq_values[:, None] * lag_values[None, :] % (2 * freqs)
    phase = turns.astype(jnp.float32) * (jnp.pi / freqs)
    return (jnp.cos(phase), jnp.sin(phase))


def lag_halves(first_freq, row_count, freqs, lag_count):
    unit_size = 64
    lag_values = jnp.arange(lag_count // 2, dtype=jnp.int32) + 1
    coarse_freq = first_freq + jnp.arange(row_count // unit_size, dtype=jnp.int32) * unit_size
    fine_freq = jnp.arange(unit_size, dtype=jnp.int32)
    coarse_cos, coarse_sin = trig_pair(coarse_freq, lag_values, freqs)
    fine_cos, fine_sin = trig_pair(fine_freq, lag_values, freqs)
    cosine = (
        coarse_cos[:, None, :] * fine_cos[None, :, :]
        - coarse_sin[:, None, :] * fine_sin[None, :, :]
    )
    sine = (
        coarse_sin[:, None, :] * fine_cos[None, :, :]
        + coarse_cos[:, None, :] * fine_sin[None, :, :]
    )
    cosine = cosine.reshape(row_count, lag_count // 2).astype(jnp.bfloat16)
    sine = sine.reshape(row_count, lag_count // 2).astype(jnp.bfloat16)
    return cosine, sine


def select_rows(block, indices):
    block_rows = block.shape[0]
    flat_block = block.reshape(block_rows, -1)
    picker = (indices[:, None] == jnp.arange(block_rows, dtype=jnp.int32)[None, :]).astype(
        jnp.bfloat16
    )
    chosen = jnp.dot(picker, flat_block, preferred_element_type=jnp.bfloat16)
    return chosen.reshape(indices.shape[0], 2, -1)


def pick_rows(block, indices):
    picker = (indices[:, None] == jnp.arange(block.shape[0], dtype=jnp.int32)[None, :]).astype(
        jnp.bfloat16
    )
    return jnp.dot(picker, block, preferred_element_type=jnp.bfloat16)


def cross_rows(near_rows, far_real, far_imag, band_gain):
    near_real = near_rows[:, 0].astype(jnp.float32)
    near_imag = near_rows[:, 1].astype(jnp.float32)
    far_real = far_real.astype(jnp.float32)
    far_imag = far_imag.astype(jnp.float32)
    real_part = (near_real * far_real + near_imag * far_imag) * band_gain
    imag_part = (near_imag * far_real - near_real * far_imag) * band_gain
    return real_part.astype(jnp.bfloat16), imag_part.astype(jnp.bfloat16)


def split_product(values, table):
    high = lax.reduce_precision(values, exponent_bits=8, mantissa_bits=7)
    low = values - high
    split = jnp.concatenate([high, low], axis=0).astype(jnp.bfloat16)
    both = jnp.dot(split, table, preferred_element_type=jnp.float32)
    return both[: values.shape[0]] + both[values.shape[0] :]


def halving_sum(parts, axis, count):
    bit = 1
    while bit < count:
        paired = parts.reshape((parts.shape[0], parts.shape[1] // 2, 2) + parts.shape[2:])
        pairs = [(i, i ^ bit) for i in range(count)]
        parts = paired[:, :, 0] + lax.ppermute(paired[:, :, 1], axis, pairs)
        bit *= 2
    return parts[:, 0]


def local(spectra, band_gain, owners, pair_near, pair_far, stack_bins):
    narrow_count = lax.axis_size("narrow")
    wide_count = lax.axis_size("wide")
    narrow_index = lax.axis_index("narrow")
    block_rows, _, freqs = spectra.shape
    steps = owners.shape[0]
    share = freqs // narrow_count
    piece = share // wide_count
    total_bins = narrow_count * wide_count * GW
    first_freq = narrow_index * share

    near = lax.dynamic_slice_in_dim(spectra, first_freq, share, axis=2)
    gain = lax.dynamic_slice_in_dim(band_gain, first_freq, share, axis=0)

    with jax.named_scope("owner_share_exchange"):
        outgoing = lax.dynamic_index_in_dim(
            spectra.reshape(block_rows, 2, narrow_count, wide_count, piece),
            narrow_index,
            2,
            keepdims=False,
        ).transpose(2, 1, 0, 3)
        arrived = lax.all_to_all(outgoing, "wide", split_axis=0, concat_axis=0, tiled=True)
        chosen = jnp.stack(
            [lax.dynamic_index_in_dim(arrived, owners[s], 0, keepdims=False) for s in range(steps)]
        )
        copies = jnp.broadcast_to(chosen[None], (wide_count,) + chosen.shape)
        gathered = lax.all_to_all(copies, "wide", split_axis=0, concat_axis=4, tiled=True)

    ids = jnp.stack([pair_near[0], pair_far[0], stack_bins[0]])
    ids = lax.all_gather(ids, "narrow", axis=2, tiled=True)
    near_ids, far_ids = ids[0], ids[1]
    bins_each = wide_count * GW
    owner_slot = lax.bitwise_xor(ids[2] // bins_each, narrow_index)
    bin_ids = owner_slot * bins_each + ids[2] % bins_each

    with jax.named_scope("cross_spectra"):
        parts = []
        for s in range(steps):
            near_rows = select_rows(near, near_ids[s])
            far_real = pick_rows(gathered[0, s, 0], far_ids[s])
            far_imag = pick_rows(gathered[0, s, 1], far_ids[s])
            parts.append(
                lax.optimization_barrier(cross_rows(near_rows, far_real, far_imag, gain))
            )

    with jax.named_scope("bin_sums"):
        real_sum = None
        imag_sum = None
        for s in range(steps):
            bin_hits = (
                jnp.arange(total_bins, dtype=jnp.int32)[:, None] == bin_ids[s][None, :]
            ).astype(jnp.bfloat16)
            real_step = jnp.dot(bin_hits, parts[s][0], preferred_element_type=jnp.float32)
            imag_step = jnp.dot(bin_hits, parts[s][1], preferred_element_type=jnp.float32)
            real_sum = real_step if real_sum is None else real_sum + real_step
            imag_sum = imag_step if imag_sum is None else imag_sum + imag_step

    with jax.named_scope("lag_product"):
        cosine, sine = lag_halves(first_freq, share, freqs, LAGS)
        even = split_product(real_sum, cosine)
        odd = split_product(imag_sum, sine)
        zero_lag = jnp.sum(real_sum, axis=1, keepdims=True)
        last = jnp.arange(LAGS // 2, dtype=jnp.int32)[None, :] == LAGS // 2 - 1
        binned = jnp.stack([even + odd, jnp.where(last, zero_lag, even - odd)])

    with jax.named_scope("bin_exchange"):
        binned = binned.reshape(2, narrow_count, wide_count * GW, LAGS // 2)
        owned = halving_sum(binned, "narrow", narrow_count)
        owned = owned.reshape(2, wide_count, GW, LAGS // 2)
        owned = lax.all_to_all(owned, "wide", split_axis=1, concat_axis=1, tiled=True)
        plus, minus = jnp.sum(owned, axis=1)
        stacked = jnp.concatenate(
            [jnp.flip(plus, axis=1), minus[:, LAGS // 2 - 1 :], minus[:, : LAGS // 2 - 1]], axis=1
        )

    inv_root = 1.0 / freqs**0.5
    stack_scale = (GW / (steps * pair_near.shape[2])) ** 0.5
    return (stacked * (inv_root * stack_scale))[None]


def solution(mesh):
    in_specs = (
        P("wide", None, None),
        P(),
        P(),
        P("wide", None, "narrow"),
        P("wide", None, "narrow"),
        P("wide", None, "narrow"),
    )
    out_specs = P("narrow", "wide", None)
    return jax.shard_map(local, mesh=mesh, in_specs=in_specs, out_specs=out_specs, check_vma=False)
```

```python
import jax
import jax.numpy as jnp
from jax import lax
from jax.sharding import PartitionSpec as P

LAGS = 1024
GW = 8


def trig_pair(freq_values, lag_values, freqs):
    turns = freq_values[:, None] * lag_values[None, :] % (2 * freqs)
    phase = turns.astype(jnp.float32) * (jnp.pi / freqs)
    return (jnp.cos(phase), jnp.sin(phase))


def lag_halves(first_freq, row_count, freqs, lag_count):
    unit_size = 64
    lag_values = jnp.arange(lag_count // 2, dtype=jnp.int32) + 1
    coarse_freq = first_freq + jnp.arange(row_count // unit_size, dtype=jnp.int32) * unit_size
    fine_freq = jnp.arange(unit_size, dtype=jnp.int32)
    coarse_cos, coarse_sin = trig_pair(coarse_freq, lag_values, freqs)
    fine_cos, fine_sin = trig_pair(fine_freq, lag_values, freqs)
    cosine = (
        coarse_cos[:, None, :] * fine_cos[None, :, :]
        - coarse_sin[:, None, :] * fine_sin[None, :, :]
    )
    sine = (
        coarse_sin[:, None, :] * fine_cos[None, :, :]
        + coarse_cos[:, None, :] * fine_sin[None, :, :]
    )
    cosine = cosine.reshape(row_count, lag_count // 2).astype(jnp.bfloat16)
    sine = sine.reshape(row_count, lag_count // 2).astype(jnp.bfloat16)
    return cosine, sine


def select_rows(block, indices):
    block_rows = block.shape[0]
    flat_block = block.reshape(block_rows, -1)
    picker = (indices[:, None] == jnp.arange(block_rows, dtype=jnp.int32)[None, :]).astype(
        jnp.bfloat16
    )
    chosen = jnp.dot(picker, flat_block, preferred_element_type=jnp.bfloat16)
    return chosen.reshape(indices.shape[0], 2, -1)


def pick_rows(block, indices):
    picker = (indices[:, None] == jnp.arange(block.shape[0], dtype=jnp.int32)[None, :]).astype(
        jnp.bfloat16
    )
    return jnp.dot(picker, block, preferred_element_type=jnp.bfloat16)


def cross_rows(near_rows, far_real, far_imag, band_gain):
    near_real = near_rows[:, 0].astype(jnp.float32)
    near_imag = near_rows[:, 1].astype(jnp.float32)
    far_real = far_real.astype(jnp.float32)
    far_imag = far_imag.astype(jnp.float32)
    real_part = (near_real * far_real + near_imag * far_imag) * band_gain
    imag_part = (near_imag * far_real - near_real * far_imag) * band_gain
    return real_part.astype(jnp.bfloat16), imag_part.astype(jnp.bfloat16)


def split_product(values, table):
    high = lax.reduce_precision(values, exponent_bits=8, mantissa_bits=7)
    low = values - high
    split = jnp.concatenate([high, low], axis=0).astype(jnp.bfloat16)
    both = jnp.dot(split, table, preferred_element_type=jnp.float32)
    return both[: values.shape[0]] + both[values.shape[0] :]


def halving_sum(parts, axis, count):
    bit = 1
    while bit < count:
        paired = parts.reshape((parts.shape[0], parts.shape[1] // 2, 2) + parts.shape[2:])
        pairs = [(i, i ^ bit) for i in range(count)]
        parts = paired[:, :, 0] + lax.ppermute(paired[:, :, 1], axis, pairs)
        bit *= 2
    return parts[:, 0]


def local(spectra, band_gain, owners, pair_near, pair_far, stack_bins):
    narrow_count = lax.axis_size("narrow")
    wide_count = lax.axis_size("wide")
    narrow_index = lax.axis_index("narrow")
    block_rows, _, freqs = spectra.shape
    steps = owners.shape[0]
    share = freqs // narrow_count
    total_bins = narrow_count * wide_count * GW
    first_freq = narrow_index * share

    near = lax.dynamic_slice_in_dim(spectra, first_freq, share, axis=2)
    gain = lax.dynamic_slice_in_dim(band_gain, first_freq, share, axis=0)

    with jax.named_scope("owner_share_exchange"):
        group = block_rows // wide_count
        outgoing = near.reshape(wide_count, group, 2, share)
        arrived = lax.all_to_all(outgoing, "wide", split_axis=0, concat_axis=0, tiled=True)
        chosen = jnp.stack(
            [lax.dynamic_index_in_dim(arrived, owners[s], 0, keepdims=False) for s in range(steps)]
        )
        copies = jnp.broadcast_to(chosen[None], (wide_count,) + chosen.shape)
        gathered = lax.all_to_all(copies, "wide", split_axis=0, concat_axis=0, tiled=True)
        far_blocks = [
            gathered[:, s].reshape(block_rows, 2, share) for s in range(steps)
        ]

    ids = jnp.stack([pair_near[0], pair_far[0], stack_bins[0]])
    ids = lax.all_gather(ids, "narrow", axis=2, tiled=True)
    near_ids, far_ids = ids[0], ids[1]
    bins_each = wide_count * GW
    owner_slot = lax.bitwise_xor(ids[2] // bins_each, narrow_index)
    bin_ids = owner_slot * bins_each + ids[2] % bins_each

    with jax.named_scope("cross_spectra"):
        parts = []
        for s in range(steps):
            near_rows = select_rows(near, near_ids[s])
            far_real = pick_rows(far_blocks[s][:, 0], far_ids[s])
            far_imag = pick_rows(far_blocks[s][:, 1], far_ids[s])
            parts.append(
                lax.optimization_barrier(cross_rows(near_rows, far_real, far_imag, gain))
            )

    with jax.named_scope("bin_sums"):
        real_sum = None
        imag_sum = None
        for s in range(steps):
            bin_hits = (
                jnp.arange(total_bins, dtype=jnp.int32)[:, None] == bin_ids[s][None, :]
            ).astype(jnp.bfloat16)
            real_step = jnp.dot(bin_hits, parts[s][0], preferred_element_type=jnp.float32)
            imag_step = jnp.dot(bin_hits, parts[s][1], preferred_element_type=jnp.float32)
            real_sum = real_step if real_sum is None else real_sum + real_step
            imag_sum = imag_step if imag_sum is None else imag_sum + imag_step

    with jax.named_scope("lag_product"):
        cosine, sine = lag_halves(first_freq, share, freqs, LAGS)
        even = split_product(real_sum, cosine)
        odd = split_product(imag_sum, sine)
        zero_lag = jnp.sum(real_sum, axis=1, keepdims=True)
        last = jnp.arange(LAGS // 2, dtype=jnp.int32)[None, :] == LAGS // 2 - 1
        binned = jnp.stack([even + odd, jnp.where(last, zero_lag, even - odd)])

    with jax.named_scope("bin_exchange"):
        binned = binned.reshape(2, narrow_count, wide_count * GW, LAGS // 2)
        owned = halving_sum(binned, "narrow", narrow_count)
        owned = owned.reshape(2, wide_count, GW, LAGS // 2)
        owned = lax.all_to_all(owned, "wide", split_axis=1, concat_axis=1, tiled=True)
        plus, minus = jnp.sum(owned, axis=1)
        stacked = jnp.concatenate(
            [jnp.flip(plus, axis=1), minus[:, LAGS // 2 - 1 :], minus[:, : LAGS // 2 - 1]], axis=1
        )

    inv_root = 1.0 / freqs**0.5
    stack_scale = (GW / (steps * pair_near.shape[2])) ** 0.5
    return (stacked * (inv_root * stack_scale))[None]


def solution(mesh):
    in_specs = (
        P("wide", None, None),
        P(),
        P(),
        P("wide", None, "narrow"),
        P("wide", None, "narrow"),
        P("wide", None, "narrow"),
    )
    out_specs = P("narrow", "wide", None)
    return jax.shard_map(local, mesh=mesh, in_specs=in_specs, out_specs=out_specs, check_vma=False)
```

```python
import jax
import jax.numpy as jnp
from jax import lax
from jax.sharding import PartitionSpec as P

LAGS = 1024
GW = 8


def trig_pair(freq_values, lag_values, freqs):
    turns = freq_values[:, None] * lag_values[None, :] % (2 * freqs)
    phase = turns.astype(jnp.float32) * (jnp.pi / freqs)
    return (jnp.cos(phase), jnp.sin(phase))


def lag_halves(first_freq, row_count, freqs, lag_count):
    unit_size = 64
    lag_values = jnp.arange(lag_count // 2, dtype=jnp.int32) + 1
    coarse_freq = first_freq + jnp.arange(row_count // unit_size, dtype=jnp.int32) * unit_size
    fine_freq = jnp.arange(unit_size, dtype=jnp.int32)
    coarse_cos, coarse_sin = trig_pair(coarse_freq, lag_values, freqs)
    fine_cos, fine_sin = trig_pair(fine_freq, lag_values, freqs)
    cosine = (
        coarse_cos[:, None, :] * fine_cos[None, :, :]
        - coarse_sin[:, None, :] * fine_sin[None, :, :]
    )
    sine = (
        coarse_sin[:, None, :] * fine_cos[None, :, :]
        + coarse_cos[:, None, :] * fine_sin[None, :, :]
    )
    cosine = cosine.reshape(row_count, lag_count // 2).astype(jnp.bfloat16)
    sine = sine.reshape(row_count, lag_count // 2).astype(jnp.bfloat16)
    return cosine, sine


def select_rows(block, indices):
    block_rows = block.shape[0]
    flat_block = block.reshape(block_rows, -1)
    picker = (indices[:, None] == jnp.arange(block_rows, dtype=jnp.int32)[None, :]).astype(
        jnp.bfloat16
    )
    chosen = jnp.dot(picker, flat_block, preferred_element_type=jnp.bfloat16)
    return chosen.reshape(indices.shape[0], 2, -1)


def pick_rows(block, indices):
    picker = (indices[:, None] == jnp.arange(block.shape[0], dtype=jnp.int32)[None, :]).astype(
        jnp.bfloat16
    )
    return jnp.dot(picker, block, preferred_element_type=jnp.bfloat16)


def cross_rows(near_rows, far_real, far_imag, band_gain):
    near_real = near_rows[:, 0].astype(jnp.float32)
    near_imag = near_rows[:, 1].astype(jnp.float32)
    far_real = far_real.astype(jnp.float32)
    far_imag = far_imag.astype(jnp.float32)
    real_part = (near_real * far_real + near_imag * far_imag) * band_gain
    imag_part = (near_imag * far_real - near_real * far_imag) * band_gain
    return real_part.astype(jnp.bfloat16), imag_part.astype(jnp.bfloat16)


def split_product(values, table):
    high = lax.reduce_precision(values, exponent_bits=8, mantissa_bits=7)
    low = values - high
    split = jnp.concatenate([high, low], axis=0).astype(jnp.bfloat16)
    both = jnp.dot(split, table, preferred_element_type=jnp.float32)
    return both[: values.shape[0]] + both[values.shape[0] :]


def halving_sum(parts, axis, count):
    bit = 1
    while bit < count:
        pairs = [(i, i ^ bit) for i in range(count)]
        parts = [
            parts[2 * j] + lax.ppermute(parts[2 * j + 1], axis, pairs)
            for j in range(len(parts) // 2)
        ]
        bit *= 2
    return parts[0]


def local(spectra, band_gain, owners, pair_near, pair_far, stack_bins):
    narrow_count = lax.axis_size("narrow")
    wide_count = lax.axis_size("wide")
    narrow_index = lax.axis_index("narrow")
    block_rows, _, freqs = spectra.shape
    steps = owners.shape[0]
    share = freqs // narrow_count
    piece = share // wide_count
    total_bins = narrow_count * wide_count * GW
    first_freq = narrow_index * share

    near = lax.dynamic_slice_in_dim(spectra, first_freq, share, axis=2)
    gain = lax.dynamic_slice_in_dim(band_gain, first_freq, share, axis=0)

    with jax.named_scope("owner_share_exchange"):
        outgoing = lax.dynamic_index_in_dim(
            spectra.reshape(block_rows, 2, narrow_count, wide_count, piece),
            narrow_index,
            2,
            keepdims=False,
        ).transpose(2, 1, 0, 3)
        arrived = lax.all_to_all(outgoing, "wide", split_axis=0, concat_axis=0, tiled=True)
        chosen = jnp.stack(
            [lax.dynamic_index_in_dim(arrived, owners[s], 0, keepdims=False) for s in range(steps)]
        )
        copies = jnp.broadcast_to(chosen[None], (wide_count,) + chosen.shape)
        gathered = lax.all_to_all(copies, "wide", split_axis=0, concat_axis=4, tiled=True)

    ids = jnp.stack([pair_near[0], pair_far[0], stack_bins[0]])
    ids = lax.all_gather(ids, "narrow", axis=2, tiled=True)
    near_ids, far_ids = ids[0], ids[1]
    bins_each = wide_count * GW
    owner_slot = lax.bitwise_xor(ids[2] // bins_each, narrow_index)
    bin_ids = owner_slot * bins_each + ids[2] % bins_each

    with jax.named_scope("cross_spectra"):
        parts = []
        for s in range(steps):
            near_rows = select_rows(near, near_ids[s])
            far_real = pick_rows(gathered[0, s, 0], far_ids[s])
            far_imag = pick_rows(gathered[0, s, 1], far_ids[s])
            parts.append(
                lax.optimization_barrier(cross_rows(near_rows, far_real, far_imag, gain))
            )

    with jax.named_scope("bin_sums"):
        real_sum = None
        imag_sum = None
        for s in range(steps):
            bin_hits = (
                jnp.arange(total_bins, dtype=jnp.int32)[:, None] == bin_ids[s][None, :]
            ).astype(jnp.bfloat16)
            real_step = jnp.dot(bin_hits, parts[s][0], preferred_element_type=jnp.float32)
            imag_step = jnp.dot(bin_hits, parts[s][1], preferred_element_type=jnp.float32)
            real_sum = real_step if real_sum is None else real_sum + real_step
            imag_sum = imag_step if imag_sum is None else imag_sum + imag_step

    with jax.named_scope("lag_product"):
        cosine, sine = lag_halves(first_freq, share, freqs, LAGS)
        last = jnp.arange(LAGS // 2, dtype=jnp.int32)[None, :] == LAGS // 2 - 1
        slots = []
        for slot in range(narrow_count):
            rows = slice(slot * bins_each, (slot + 1) * bins_each)
            even = split_product(real_sum[rows], cosine)
            odd = split_product(imag_sum[rows], sine)
            zero_lag = jnp.sum(real_sum[rows], axis=1, keepdims=True)
            slots.append(jnp.stack([even + odd, jnp.where(last, zero_lag, even - odd)]))

    with jax.named_scope("bin_exchange"):
        owned = halving_sum(slots, "narrow", narrow_count)
        owned = owned.reshape(2, wide_count, GW, LAGS // 2)
        owned = lax.all_to_all(owned, "wide", split_axis=1, concat_axis=1, tiled=True)
        plus, minus = jnp.sum(owned, axis=1)
        stacked = jnp.concatenate(
            [jnp.flip(plus, axis=1), minus[:, LAGS // 2 - 1 :], minus[:, : LAGS // 2 - 1]], axis=1
        )

    inv_root = 1.0 / freqs**0.5
    stack_scale = (GW / (steps * pair_near.shape[2])) ** 0.5
    return (stacked * (inv_root * stack_scale))[None]


def solution(mesh):
    in_specs = (
        P("wide", None, None),
        P(),
        P(),
        P("wide", None, "narrow"),
        P("wide", None, "narrow"),
        P("wide", None, "narrow"),
    )
    out_specs = P("narrow", "wide", None)
    return jax.shard_map(local, mesh=mesh, in_specs=in_specs, out_specs=out_specs, check_vma=False)
```

```python
import jax
import jax.numpy as jnp
from jax import lax
from jax.sharding import PartitionSpec as P

LAGS = 1024
GW = 8


def trig_pair(freq_values, lag_values, freqs):
    turns = freq_values[:, None] * lag_values[None, :] % (2 * freqs)
    phase = turns.astype(jnp.float32) * (jnp.pi / freqs)
    return (jnp.cos(phase), jnp.sin(phase))


def lag_halves(first_freq, row_count, freqs, lag_count):
    unit_size = 64
    lag_values = jnp.arange(lag_count // 2, dtype=jnp.int32) + 1
    coarse_freq = first_freq + jnp.arange(row_count // unit_size, dtype=jnp.int32) * unit_size
    fine_freq = jnp.arange(unit_size, dtype=jnp.int32)
    coarse_cos, coarse_sin = trig_pair(coarse_freq, lag_values, freqs)
    fine_cos, fine_sin = trig_pair(fine_freq, lag_values, freqs)
    cosine = (
        coarse_cos[:, None, :] * fine_cos[None, :, :]
        - coarse_sin[:, None, :] * fine_sin[None, :, :]
    )
    sine = (
        coarse_sin[:, None, :] * fine_cos[None, :, :]
        + coarse_cos[:, None, :] * fine_sin[None, :, :]
    )
    cosine = cosine.reshape(row_count, lag_count // 2).astype(jnp.bfloat16)
    sine = sine.reshape(row_count, lag_count // 2).astype(jnp.bfloat16)
    return cosine, sine


def select_rows(block, indices):
    block_rows = block.shape[0]
    flat_block = block.reshape(block_rows, -1)
    picker = (indices[:, None] == jnp.arange(block_rows, dtype=jnp.int32)[None, :]).astype(
        jnp.bfloat16
    )
    chosen = jnp.dot(picker, flat_block, preferred_element_type=jnp.bfloat16)
    return chosen.reshape(indices.shape[0], 2, -1)


def pick_rows(block, indices):
    picker = (indices[:, None] == jnp.arange(block.shape[0], dtype=jnp.int32)[None, :]).astype(
        jnp.bfloat16
    )
    return jnp.dot(picker, block, preferred_element_type=jnp.bfloat16)


def cross_rows(near_rows, far_real, far_imag, band_gain):
    near_real = near_rows[:, 0].astype(jnp.float32)
    near_imag = near_rows[:, 1].astype(jnp.float32)
    far_real = far_real.astype(jnp.float32)
    far_imag = far_imag.astype(jnp.float32)
    real_part = (near_real * far_real + near_imag * far_imag) * band_gain
    imag_part = (near_imag * far_real - near_real * far_imag) * band_gain
    return real_part.astype(jnp.bfloat16), imag_part.astype(jnp.bfloat16)


def split_product(values, table):
    high = lax.reduce_precision(values, exponent_bits=8, mantissa_bits=7)
    low = values - high
    split = jnp.concatenate([high, low], axis=0).astype(jnp.bfloat16)
    both = jnp.dot(split, table, preferred_element_type=jnp.float32)
    return both[: values.shape[0]] + both[values.shape[0] :]


def halving_sum(parts, axis, count):
    bit = 1
    while bit < count:
        paired = parts.reshape((parts.shape[0], parts.shape[1] // 2, 2) + parts.shape[2:])
        pairs = [(i, i ^ bit) for i in range(count)]
        parts = paired[:, :, 0] + lax.ppermute(paired[:, :, 1], axis, pairs)
        bit *= 2
    return parts[:, 0]


def local(spectra, band_gain, owners, pair_near, pair_far, stack_bins):
    narrow_count = lax.axis_size("narrow")
    wide_count = lax.axis_size("wide")
    narrow_index = lax.axis_index("narrow")
    block_rows, _, freqs = spectra.shape
    steps = owners.shape[0]
    share = freqs // narrow_count
    piece = share // wide_count
    total_bins = narrow_count * wide_count * GW
    first_freq = narrow_index * share

    near = lax.dynamic_slice_in_dim(spectra, first_freq, share, axis=2)
    gain = lax.dynamic_slice_in_dim(band_gain, first_freq, share, axis=0)

    with jax.named_scope("owner_share_exchange"):
        outgoing = lax.dynamic_index_in_dim(
            spectra.reshape(block_rows, 2, narrow_count, wide_count, piece),
            narrow_index,
            2,
            keepdims=False,
        ).transpose(2, 1, 0, 3)
        arrived = lax.all_to_all(outgoing, "wide", split_axis=0, concat_axis=0, tiled=True)
        copies = arrived[jnp.broadcast_to(owners[None, :], (wide_count, steps))]
        gathered = lax.all_to_all(copies, "wide", split_axis=0, concat_axis=4, tiled=True)

    ids = jnp.stack([pair_near[0], pair_far[0], stack_bins[0]])
    ids = lax.all_gather(ids, "narrow", axis=2, tiled=True)
    near_ids, far_ids = ids[0], ids[1]
    bins_each = wide_count * GW
    owner_slot = lax.bitwise_xor(ids[2] // bins_each, narrow_index)
    bin_ids = owner_slot * bins_each + ids[2] % bins_each

    with jax.named_scope("cross_spectra"):
        parts = []
        for s in range(steps):
            near_rows = select_rows(near, near_ids[s])
            far_real = pick_rows(gathered[0, s, 0], far_ids[s])
            far_imag = pick_rows(gathered[0, s, 1], far_ids[s])
            parts.append(
                lax.optimization_barrier(cross_rows(near_rows, far_real, far_imag, gain))
            )

    with jax.named_scope("bin_sums"):
        real_sum = None
        imag_sum = None
        for s in range(steps):
            bin_hits = (
                jnp.arange(total_bins, dtype=jnp.int32)[:, None] == bin_ids[s][None, :]
            ).astype(jnp.bfloat16)
            real_step = jnp.dot(bin_hits, parts[s][0], preferred_element_type=jnp.float32)
            imag_step = jnp.dot(bin_hits, parts[s][1], preferred_element_type=jnp.float32)
            real_sum = real_step if real_sum is None else real_sum + real_step
            imag_sum = imag_step if imag_sum is None else imag_sum + imag_step

    with jax.named_scope("lag_product"):
        cosine, sine = lag_halves(first_freq, share, freqs, LAGS)
        even = split_product(real_sum, cosine)
        odd = split_product(imag_sum, sine)
        zero_lag = jnp.sum(real_sum, axis=1, keepdims=True)
        last = jnp.arange(LAGS // 2, dtype=jnp.int32)[None, :] == LAGS // 2 - 1
        binned = jnp.stack([even + odd, jnp.where(last, zero_lag, even - odd)])

    with jax.named_scope("bin_exchange"):
        binned = binned.reshape(2, narrow_count, wide_count * GW, LAGS // 2)
        owned = halving_sum(binned, "narrow", narrow_count)
        owned = owned.reshape(2, wide_count, GW, LAGS // 2)
        owned = lax.all_to_all(owned, "wide", split_axis=1, concat_axis=1, tiled=True)
        plus, minus = jnp.sum(owned, axis=1)
        stacked = jnp.concatenate(
            [jnp.flip(plus, axis=1), minus[:, LAGS // 2 - 1 :], minus[:, : LAGS // 2 - 1]], axis=1
        )

    inv_root = 1.0 / freqs**0.5
    stack_scale = (GW / (steps * pair_near.shape[2])) ** 0.5
    return (stacked * (inv_root * stack_scale))[None]


def solution(mesh):
    in_specs = (
        P("wide", None, None),
        P(),
        P(),
        P("wide", None, "narrow"),
        P("wide", None, "narrow"),
        P("wide", None, "narrow"),
    )
    out_specs = P("narrow", "wide", None)
    return jax.shard_map(local, mesh=mesh, in_specs=in_specs, out_specs=out_specs, check_vma=False)
```

```python
import jax
import jax.numpy as jnp
from jax import lax
from jax.sharding import PartitionSpec as P

LAGS = 1024
GW = 8


def trig_pair(freq_values, lag_values, freqs):
    turns = freq_values[:, None] * lag_values[None, :] % (2 * freqs)
    phase = turns.astype(jnp.float32) * (jnp.pi / freqs)
    return (jnp.cos(phase), jnp.sin(phase))


def lag_halves(first_freq, row_count, freqs, lag_count):
    unit_size = 64
    lag_values = jnp.arange(lag_count // 2, dtype=jnp.int32) + 1
    coarse_freq = first_freq + jnp.arange(row_count // unit_size, dtype=jnp.int32) * unit_size
    fine_freq = jnp.arange(unit_size, dtype=jnp.int32)
    coarse_cos, coarse_sin = trig_pair(coarse_freq, lag_values, freqs)
    fine_cos, fine_sin = trig_pair(fine_freq, lag_values, freqs)
    cosine = (
        coarse_cos[:, None, :] * fine_cos[None, :, :]
        - coarse_sin[:, None, :] * fine_sin[None, :, :]
    )
    sine = (
        coarse_sin[:, None, :] * fine_cos[None, :, :]
        + coarse_cos[:, None, :] * fine_sin[None, :, :]
    )
    cosine = cosine.reshape(row_count, lag_count // 2).astype(jnp.bfloat16)
    sine = sine.reshape(row_count, lag_count // 2).astype(jnp.bfloat16)
    return cosine, sine


def select_rows(block, indices):
    block_rows = block.shape[0]
    flat_block = block.reshape(block_rows, -1)
    picker = (indices[:, None] == jnp.arange(block_rows, dtype=jnp.int32)[None, :]).astype(
        jnp.bfloat16
    )
    chosen = jnp.dot(picker, flat_block, preferred_element_type=jnp.bfloat16)
    return chosen.reshape(indices.shape[0], 2, -1)


def pick_rows(block, indices):
    picker = (indices[:, None] == jnp.arange(block.shape[0], dtype=jnp.int32)[None, :]).astype(
        jnp.bfloat16
    )
    return jnp.dot(picker, block, preferred_element_type=jnp.bfloat16)


def cross_rows(near_rows, far_real, far_imag, band_gain):
    near_real = near_rows[:, 0].astype(jnp.float32)
    near_imag = near_rows[:, 1].astype(jnp.float32)
    far_real = far_real.astype(jnp.float32)
    far_imag = far_imag.astype(jnp.float32)
    real_part = (near_real * far_real + near_imag * far_imag) * band_gain
    imag_part = (near_imag * far_real - near_real * far_imag) * band_gain
    return real_part.astype(jnp.bfloat16), imag_part.astype(jnp.bfloat16)


def split_product(values, table):
    high = lax.reduce_precision(values, exponent_bits=8, mantissa_bits=7)
    low = values - high
    split = jnp.concatenate([high, low], axis=0).astype(jnp.bfloat16)
    both = jnp.dot(split, table, preferred_element_type=jnp.float32)
    return both[: values.shape[0]] + both[values.shape[0] :]


def halving_sum(parts, axis, count):
    bit = 1
    while bit < count:
        paired = parts.reshape((parts.shape[0], parts.shape[1] // 2, 2) + parts.shape[2:])
        pairs = [(i, i ^ bit) for i in range(count)]
        parts = paired[:, :, 0] + lax.ppermute(paired[:, :, 1], axis, pairs)
        bit *= 2
    return parts[:, 0]


def local(spectra, band_gain, owners, pair_near, pair_far, stack_bins):
    narrow_count = lax.axis_size("narrow")
    wide_count = lax.axis_size("wide")
    narrow_index = lax.axis_index("narrow")
    block_rows, _, freqs = spectra.shape
    steps = owners.shape[0]
    share = freqs // narrow_count
    piece = share // wide_count
    total_bins = narrow_count * wide_count * GW
    first_freq = narrow_index * share

    near = lax.dynamic_slice_in_dim(spectra, first_freq, share, axis=2)
    gain = lax.dynamic_slice_in_dim(band_gain, first_freq, share, axis=0)

    with jax.named_scope("owner_share_exchange"):
        outgoing = lax.dynamic_index_in_dim(
            spectra.reshape(block_rows, 2, narrow_count, wide_count, piece),
            narrow_index,
            2,
            keepdims=False,
        ).transpose(2, 1, 0, 3)
        arrived = lax.all_to_all(outgoing, "wide", split_axis=0, concat_axis=0, tiled=True)
        chosen = jnp.stack(
            [lax.dynamic_index_in_dim(arrived, owners[s], 0, keepdims=False) for s in range(steps)]
        )
        copies = jnp.broadcast_to(chosen[None], (wide_count,) + chosen.shape)
        gathered = lax.all_to_all(copies, "wide", split_axis=0, concat_axis=4, tiled=True)

    ids = jnp.stack([pair_near[0], pair_far[0], stack_bins[0]])
    ids = lax.all_gather(ids, "narrow", axis=2, tiled=True)
    near_ids, far_ids = ids[0], ids[1]
    bins_each = wide_count * GW
    owner_slot = lax.bitwise_xor(ids[2] // bins_each, narrow_index)
    bin_ids = owner_slot * bins_each + ids[2] % bins_each

    with jax.named_scope("cross_spectra"):
        parts = []
        for s in range(steps):
            near_rows = select_rows(near, near_ids[s])
            picker = (
                far_ids[s][:, None] == jnp.arange(block_rows, dtype=jnp.int32)[None, :]
            ).astype(jnp.bfloat16)
            far_real, far_imag = jnp.einsum(
                "pc,rcf->rpf", picker, gathered[0, s], preferred_element_type=jnp.bfloat16
            )
            parts.append(
                lax.optimization_barrier(cross_rows(near_rows, far_real, far_imag, gain))
            )

    with jax.named_scope("bin_sums"):
        real_sum = None
        imag_sum = None
        for s in range(steps):
            bin_hits = (
                jnp.arange(total_bins, dtype=jnp.int32)[:, None] == bin_ids[s][None, :]
            ).astype(jnp.bfloat16)
            real_step = jnp.dot(bin_hits, parts[s][0], preferred_element_type=jnp.float32)
            imag_step = jnp.dot(bin_hits, parts[s][1], preferred_element_type=jnp.float32)
            real_sum = real_step if real_sum is None else real_sum + real_step
            imag_sum = imag_step if imag_sum is None else imag_sum + imag_step

    with jax.named_scope("lag_product"):
        cosine, sine = lag_halves(first_freq, share, freqs, LAGS)
        even = split_product(real_sum, cosine)
        odd = split_product(imag_sum, sine)
        zero_lag = jnp.sum(real_sum, axis=1, keepdims=True)
        last = jnp.arange(LAGS // 2, dtype=jnp.int32)[None, :] == LAGS // 2 - 1
        binned = jnp.stack([even + odd, jnp.where(last, zero_lag, even - odd)])

    with jax.named_scope("bin_exchange"):
        binned = binned.reshape(2, narrow_count, wide_count * GW, LAGS // 2)
        owned = halving_sum(binned, "narrow", narrow_count)
        owned = owned.reshape(2, wide_count, GW, LAGS // 2)
        owned = lax.all_to_all(owned, "wide", split_axis=1, concat_axis=1, tiled=True)
        plus, minus = jnp.sum(owned, axis=1)
        stacked = jnp.concatenate(
            [jnp.flip(plus, axis=1), minus[:, LAGS // 2 - 1 :], minus[:, : LAGS // 2 - 1]], axis=1
        )

    inv_root = 1.0 / freqs**0.5
    stack_scale = (GW / (steps * pair_near.shape[2])) ** 0.5
    return (stacked * (inv_root * stack_scale))[None]


def solution(mesh):
    in_specs = (
        P("wide", None, None),
        P(),
        P(),
        P("wide", None, "narrow"),
        P("wide", None, "narrow"),
        P("wide", None, "narrow"),
    )
    out_specs = P("narrow", "wide", None)
    return jax.shard_map(local, mesh=mesh, in_specs=in_specs, out_specs=out_specs, check_vma=False)
```

```python
import jax
import jax.numpy as jnp
from jax import lax
from jax.sharding import PartitionSpec as P

LAGS = 1024
GW = 8


def trig_pair(freq_values, lag_values, freqs):
    turns = freq_values[:, None] * lag_values[None, :] % (2 * freqs)
    phase = turns.astype(jnp.float32) * (jnp.pi / freqs)
    return (jnp.cos(phase), jnp.sin(phase))


def lag_halves(first_freq, row_count, freqs, lag_count):
    unit_size = 64
    lag_values = jnp.arange(lag_count // 2, dtype=jnp.int32) + 1
    coarse_freq = first_freq + jnp.arange(row_count // unit_size, dtype=jnp.int32) * unit_size
    fine_freq = jnp.arange(unit_size, dtype=jnp.int32)
    coarse_cos, coarse_sin = trig_pair(coarse_freq, lag_values, freqs)
    fine_cos, fine_sin = trig_pair(fine_freq, lag_values, freqs)
    cosine = (
        coarse_cos[:, None, :] * fine_cos[None, :, :]
        - coarse_sin[:, None, :] * fine_sin[None, :, :]
    )
    sine = (
        coarse_sin[:, None, :] * fine_cos[None, :, :]
        + coarse_cos[:, None, :] * fine_sin[None, :, :]
    )
    cosine = cosine.reshape(row_count, lag_count // 2).astype(jnp.bfloat16)
    sine = sine.reshape(row_count, lag_count // 2).astype(jnp.bfloat16)
    return cosine, sine


def select_rows(block, indices):
    block_rows = block.shape[0]
    flat_block = block.reshape(block_rows, -1)
    picker = (indices[:, None] == jnp.arange(block_rows, dtype=jnp.int32)[None, :]).astype(
        jnp.bfloat16
    )
    chosen = jnp.dot(picker, flat_block, preferred_element_type=jnp.bfloat16)
    return chosen.reshape(indices.shape[0], 2, -1)


def pick_rows(block, indices):
    picker = (indices[:, None] == jnp.arange(block.shape[0], dtype=jnp.int32)[None, :]).astype(
        jnp.bfloat16
    )
    return jnp.dot(picker, block, preferred_element_type=jnp.bfloat16)


def cross_rows(near_rows, far_real, far_imag, band_gain):
    near_real = near_rows[:, 0].astype(jnp.float32)
    near_imag = near_rows[:, 1].astype(jnp.float32)
    far_real = far_real.astype(jnp.float32)
    far_imag = far_imag.astype(jnp.float32)
    real_part = (near_real * far_real + near_imag * far_imag) * band_gain
    imag_part = (near_imag * far_real - near_real * far_imag) * band_gain
    return real_part.astype(jnp.bfloat16), imag_part.astype(jnp.bfloat16)


def split_product(values, table):
    high = lax.reduce_precision(values, exponent_bits=8, mantissa_bits=7)
    low = values - high
    split = jnp.concatenate([high, low], axis=0).astype(jnp.bfloat16)
    both = jnp.dot(split, table, preferred_element_type=jnp.float32)
    return both[: values.shape[0]] + both[values.shape[0] :]


def halving_sum(parts, axis, count):
    bit = 1
    while bit < count:
        paired = parts.reshape((parts.shape[0], parts.shape[1] // 2, 2) + parts.shape[2:])
        pairs = [(i, i ^ bit) for i in range(count)]
        parts = paired[:, :, 0] + lax.ppermute(paired[:, :, 1], axis, pairs)
        bit *= 2
    return parts[:, 0]


def local(spectra, band_gain, owners, pair_near, pair_far, stack_bins):
    narrow_count = lax.axis_size("narrow")
    wide_count = lax.axis_size("wide")
    narrow_index = lax.axis_index("narrow")
    block_rows, _, freqs = spectra.shape
    steps = owners.shape[0]
    share = freqs // narrow_count
    piece = share // wide_count
    total_bins = narrow_count * wide_count * GW
    first_freq = narrow_index * share

    near = lax.dynamic_slice_in_dim(spectra, first_freq, share, axis=2)
    gain = lax.dynamic_slice_in_dim(band_gain, first_freq, share, axis=0)

    with jax.named_scope("owner_share_exchange"):
        outgoing = lax.dynamic_index_in_dim(
            spectra.reshape(block_rows, 2, narrow_count, wide_count, piece),
            narrow_index,
            2,
            keepdims=False,
        ).transpose(2, 1, 0, 3)
        arrived = lax.all_to_all(outgoing, "wide", split_axis=0, concat_axis=0, tiled=True)
        chosen = jnp.stack(
            [lax.dynamic_index_in_dim(arrived, owners[s], 0, keepdims=False) for s in range(steps)]
        )
        copies = jnp.broadcast_to(chosen[None], (wide_count,) + chosen.shape)
        gathered = lax.all_to_all(copies, "wide", split_axis=0, concat_axis=4, tiled=True)

    ids = jnp.stack([pair_near[0], pair_far[0], stack_bins[0]])
    ids = lax.all_gather(ids, "narrow", axis=2, tiled=True)
    near_ids, far_ids = ids[0], ids[1]
    bins_each = wide_count * GW
    owner_slot = lax.bitwise_xor(ids[2] // bins_each, narrow_index)
    bin_ids = owner_slot * bins_each + ids[2] % bins_each

    with jax.named_scope("cross_spectra"):
        parts = []
        for s in range(steps):
            near_rows = select_rows(near, near_ids[s])
            far_real = pick_rows(gathered[0, s, 0], far_ids[s])
            far_imag = pick_rows(gathered[0, s, 1], far_ids[s])
            parts.append(cross_rows(near_rows, far_real, far_imag, gain))

    with jax.named_scope("bin_sums"):
        real_sum = None
        imag_sum = None
        for s in range(steps):
            bin_hits = (
                jnp.arange(total_bins, dtype=jnp.int32)[:, None] == bin_ids[s][None, :]
            ).astype(jnp.bfloat16)
            real_step = jnp.dot(bin_hits, parts[s][0], preferred_element_type=jnp.float32)
            imag_step = jnp.dot(bin_hits, parts[s][1], preferred_element_type=jnp.float32)
            real_sum = real_step if real_sum is None else real_sum + real_step
            imag_sum = imag_step if imag_sum is None else imag_sum + imag_step

    with jax.named_scope("lag_product"):
        cosine, sine = lag_halves(first_freq, share, freqs, LAGS)
        even = split_product(real_sum, cosine)
        odd = split_product(imag_sum, sine)
        zero_lag = jnp.sum(real_sum, axis=1, keepdims=True)
        last = jnp.arange(LAGS // 2, dtype=jnp.int32)[None, :] == LAGS // 2 - 1
        binned = jnp.stack([even + odd, jnp.where(last, zero_lag, even - odd)])

    with jax.named_scope("bin_exchange"):
        binned = binned.reshape(2, narrow_count, wide_count * GW, LAGS // 2)
        owned = halving_sum(binned, "narrow", narrow_count)
        owned = owned.reshape(2, wide_count, GW, LAGS // 2)
        owned = lax.all_to_all(owned, "wide", split_axis=1, concat_axis=1, tiled=True)
        plus, minus = jnp.sum(owned, axis=1)
        stacked = jnp.concatenate(
            [jnp.flip(plus, axis=1), minus[:, LAGS // 2 - 1 :], minus[:, : LAGS // 2 - 1]], axis=1
        )

    inv_root = 1.0 / freqs**0.5
    stack_scale = (GW / (steps * pair_near.shape[2])) ** 0.5
    return (stacked * (inv_root * stack_scale))[None]


def solution(mesh):
    in_specs = (
        P("wide", None, None),
        P(),
        P(),
        P("wide", None, "narrow"),
        P("wide", None, "narrow"),
        P("wide", None, "narrow"),
    )
    out_specs = P("narrow", "wide", None)
    return jax.shard_map(local, mesh=mesh, in_specs=in_specs, out_specs=out_specs, check_vma=False)
```

```python
import jax
import jax.numpy as jnp
from jax import lax
from jax.sharding import PartitionSpec as P

LAGS = 1024
GW = 8


def trig_pair(freq_values, lag_values, freqs):
    turns = freq_values[:, None] * lag_values[None, :] % (2 * freqs)
    phase = turns.astype(jnp.float32) * (jnp.pi / freqs)
    return (jnp.cos(phase), jnp.sin(phase))


def lag_halves(first_freq, row_count, freqs, lag_count):
    unit_size = 64
    lag_values = jnp.arange(lag_count // 2, dtype=jnp.int32) + 1
    coarse_freq = first_freq + jnp.arange(row_count // unit_size, dtype=jnp.int32) * unit_size
    fine_freq = jnp.arange(unit_size, dtype=jnp.int32)
    coarse_cos, coarse_sin = trig_pair(coarse_freq, lag_values, freqs)
    fine_cos, fine_sin = trig_pair(fine_freq, lag_values, freqs)
    cosine = (
        coarse_cos[:, None, :] * fine_cos[None, :, :]
        - coarse_sin[:, None, :] * fine_sin[None, :, :]
    )
    sine = (
        coarse_sin[:, None, :] * fine_cos[None, :, :]
        + coarse_cos[:, None, :] * fine_sin[None, :, :]
    )
    cosine = cosine.reshape(row_count, lag_count // 2).astype(jnp.bfloat16)
    sine = sine.reshape(row_count, lag_count // 2).astype(jnp.bfloat16)
    return cosine, sine


def select_rows(block, indices):
    block_rows = block.shape[0]
    flat_block = block.reshape(block_rows, -1)
    picker = (indices[:, None] == jnp.arange(block_rows, dtype=jnp.int32)[None, :]).astype(
        jnp.bfloat16
    )
    chosen = jnp.dot(picker, flat_block, preferred_element_type=jnp.bfloat16)
    return chosen.reshape(indices.shape[0], 2, -1)


def pick_rows(block, indices):
    picker = (indices[:, None] == jnp.arange(block.shape[0], dtype=jnp.int32)[None, :]).astype(
        jnp.bfloat16
    )
    return jnp.dot(picker, block, preferred_element_type=jnp.bfloat16)


def cross_rows(near_rows, far_real, far_imag, band_gain):
    near_real = near_rows[:, 0].astype(jnp.float32)
    near_imag = near_rows[:, 1].astype(jnp.float32)
    far_real = far_real.astype(jnp.float32)
    far_imag = far_imag.astype(jnp.float32)
    real_part = (near_real * far_real + near_imag * far_imag) * band_gain
    imag_part = (near_imag * far_real - near_real * far_imag) * band_gain
    return real_part.astype(jnp.bfloat16), imag_part.astype(jnp.bfloat16)


def split_product(values, table):
    high = lax.reduce_precision(values, exponent_bits=8, mantissa_bits=7)
    low = values - high
    split = jnp.concatenate([high, low], axis=0).astype(jnp.bfloat16)
    both = jnp.dot(split, table, preferred_element_type=jnp.float32)
    return both[: values.shape[0]] + both[values.shape[0] :]


def halving_sum(parts, axis, count):
    bit = 1
    while bit < count:
        paired = parts.reshape((parts.shape[0], parts.shape[1] // 2, 2) + parts.shape[2:])
        pairs = [(i, i ^ bit) for i in range(count)]
        parts = paired[:, :, 0] + lax.ppermute(paired[:, :, 1], axis, pairs)
        bit *= 2
    return parts[:, 0]


def local(spectra, band_gain, owners, pair_near, pair_far, stack_bins):
    narrow_count = lax.axis_size("narrow")
    wide_count = lax.axis_size("wide")
    narrow_index = lax.axis_index("narrow")
    block_rows, _, freqs = spectra.shape
    steps = owners.shape[0]
    share = freqs // narrow_count
    piece = share // wide_count
    total_bins = narrow_count * wide_count * GW
    first_freq = narrow_index * share

    near = lax.dynamic_slice_in_dim(spectra, first_freq, share, axis=2)
    gain = lax.dynamic_slice_in_dim(band_gain, first_freq, share, axis=0)

    with jax.named_scope("owner_share_exchange"):
        outgoing = lax.dynamic_index_in_dim(
            spectra.reshape(block_rows, 2, narrow_count, wide_count, piece),
            narrow_index,
            2,
            keepdims=False,
        ).transpose(2, 1, 0, 3)
        arrived = lax.all_to_all(outgoing, "wide", split_axis=0, concat_axis=0, tiled=True)
        chosen = jnp.stack(
            [lax.dynamic_index_in_dim(arrived, owners[s], 0, keepdims=False) for s in range(steps)]
        )
        copies = jnp.broadcast_to(chosen[None], (wide_count,) + chosen.shape)
        gathered = lax.all_to_all(copies, "wide", split_axis=0, concat_axis=4, tiled=True)

    ids = jnp.stack([pair_near[0], pair_far[0], stack_bins[0]])
    ids = lax.all_gather(ids, "narrow", axis=2, tiled=True)
    near_ids, far_ids = ids[0], ids[1]
    bins_each = wide_count * GW
    owner_slot = lax.bitwise_xor(ids[2] // bins_each, narrow_index)
    bin_ids = owner_slot * bins_each + ids[2] % bins_each

    with jax.named_scope("cross_spectra"):
        parts = []
        for s in range(steps):
            near_rows = select_rows(near, near_ids[s])
            picker = (
                far_ids[s][:, None] == jnp.arange(block_rows, dtype=jnp.int32)[None, :]
            ).astype(jnp.bfloat16)
            far_real, far_imag = jnp.einsum(
                "pc,rcf->rpf", picker, gathered[0, s], preferred_element_type=jnp.bfloat16
            )
            parts.append(cross_rows(near_rows, far_real, far_imag, gain))

    with jax.named_scope("bin_sums"):
        real_sum = None
        imag_sum = None
        for s in range(steps):
            bin_hits = (
                jnp.arange(total_bins, dtype=jnp.int32)[:, None] == bin_ids[s][None, :]
            ).astype(jnp.bfloat16)
            real_step = jnp.dot(bin_hits, parts[s][0], preferred_element_type=jnp.float32)
            imag_step = jnp.dot(bin_hits, parts[s][1], preferred_element_type=jnp.float32)
            real_sum = real_step if real_sum is None else real_sum + real_step
            imag_sum = imag_step if imag_sum is None else imag_sum + imag_step

    with jax.named_scope("lag_product"):
        cosine, sine = lag_halves(first_freq, share, freqs, LAGS)
        even = split_product(real_sum, cosine)
        odd = split_product(imag_sum, sine)
        zero_lag = jnp.sum(real_sum, axis=1, keepdims=True)
        last = jnp.arange(LAGS // 2, dtype=jnp.int32)[None, :] == LAGS // 2 - 1
        binned = jnp.stack([even + odd, jnp.where(last, zero_lag, even - odd)])

    with jax.named_scope("bin_exchange"):
        binned = binned.reshape(2, narrow_count, wide_count * GW, LAGS // 2)
        owned = halving_sum(binned, "narrow", narrow_count)
        owned = owned.reshape(2, wide_count, GW, LAGS // 2)
        owned = lax.all_to_all(owned, "wide", split_axis=1, concat_axis=1, tiled=True)
        plus, minus = jnp.sum(owned, axis=1)
        stacked = jnp.concatenate(
            [jnp.flip(plus, axis=1), minus[:, LAGS // 2 - 1 :], minus[:, : LAGS // 2 - 1]], axis=1
        )

    inv_root = 1.0 / freqs**0.5
    stack_scale = (GW / (steps * pair_near.shape[2])) ** 0.5
    return (stacked * (inv_root * stack_scale))[None]


def solution(mesh):
    in_specs = (
        P("wide", None, None),
        P(),
        P(),
        P("wide", None, "narrow"),
        P("wide", None, "narrow"),
        P("wide", None, "narrow"),
    )
    out_specs = P("narrow", "wide", None)
    return jax.shard_map(local, mesh=mesh, in_specs=in_specs, out_specs=out_specs, check_vma=False)
```
